32 devices in a mesh: grp: 2 (over y), seq: 16 (over z, x, core).
Axes of the slice: x: 2, y: 2, z: 4, core: 2. Of those that a mesh axis runs over, the one named last changes fastest.
Arguments:
- ssm_in: bfloat16 [2048, 4096], P(('grp', 'seq')), parts along dimension 0
- ssm_dt: bfloat16 [2048, 4096], P(('grp', 'seq')), parts along dimension 0, as said below
- ssm_a: float32 [16, 4096], replicated, as said below
- ssm_b: float32 [16, 2048], P(None, ('grp', 'seq')), parts along dimension 1, may hold values from -0.1875 to 0.1875
- ssm_c: float32 [16, 2048], P(None, ('grp', 'seq')), parts along dimension 1, may hold values from -1.5 to 1.5
- attn_q: bfloat16 [2048, 4096], P(('grp', 'seq')), parts along dimension 0
- attn_kv: bfloat16 [2048, 2048], P(('grp', 'seq')), parts along dimension 0
- moe_in: bfloat16 [2048, 4096], P(('grp', 'seq')), parts along dimension 0, may hold values from -6 to 6
- moe_routes: int32 [2048, 2], P(('grp', 'seq')), parts along dimension 0, may hold values from 0 to 15, all different within a row; in each aligned block of 64 rows (0 to 63, 64 to 127, ...) at most 12 rows name the same one
- moe_prob: float32 [2048, 2], P(('grp', 'seq')), parts along dimension 0, may hold values from 0.2 to 1
- w_gate: bfloat16 [4096, 4096], P(None, 'seq'), may hold values from -0.09375 to 0.09375
- w_up: bfloat16 [4096, 4096], P(None, 'seq'), may hold values from -0.09375 to 0.09375
- w_down: bfloat16 [4096, 4096], P('seq'), may hold values from -0.1875 to 0.1875
Outputs:
- ssm_out: bfloat16 [2048, 4096], P(('grp', 'seq')), parts along dimension 0
- attn_out: bfloat16 [2048, 4096], P(('grp', 'seq')), parts along dimension 0
- moe_out: bfloat16 [2048, 4096], P(('grp', 'seq')), parts along dimension 0
The draws below stay inside these ranges and needn't reach their ends.
There are 2 independent parts, one for each index of `grp`. The reference program is written for one: setup_inputs(seed, part) draws one part's arguments, and reference() takes and returns one part's arrays. A program takes and returns all parts, laid end to end along the dimension named above; an argument that names none is the same for every part. Nothing has to cross between parts.
Inputs may be any that keep to these rules, and one draw needn't show every extreme that they name: `moe_routes`: no expert is named by more than 12 positions of one device; a position's two experts differ. `ssm_dt`: Positive. `ssm_a`: Negative.
All inputs are finite; a program needn't handle non-finite values.
Results may differ from the reference program's by a relative error of at most 0.0079.
Values may be sent and summed in bfloat16 or wider, within the bound.
No kernel may reach another device: no remote copies, remote signals or barrier semaphores. Data moves between devices by JAX's collectives and lax.ppermute only.
A program may use at most 192 MiB of HBM per device.

```python
import math
import jax
import jax.numpy as jnp
import numpy as np
from jax import lax

TOK_DEV = 64
CH = 4096
NS = 16
D = 4096
HQ = 32
HK = 8
HEAD_SIZE = 128
EXPERTS = 16
EXP_WIN = 4
FF_DEV = 256
TOKENS = 1024
GROUP = 4
FF_EXP = 1024
CAP = 12
N_SEQ = 16


def cluster_rows(key):
    chosen_rows = jax.random.randint(jax.random.fold_in(key, 7), (2,), 0, TOKENS)
    positions = jnp.arange(TOKENS)
    return (positions == chosen_rows[0]) | (positions == chosen_rows[1])


def draw_ssm_in(key, part):
    marked_rows = cluster_rows(key)
    noise = jnp.clip(jax.random.normal(jax.random.fold_in(key, 1), (TOKENS, CH)), -6.0, 6.0)
    return jnp.where(marked_rows[:, None], noise / TOKENS, noise).astype(jnp.bfloat16)


def draw_ssm_dt(key, part):
    marked_rows = cluster_rows(key)
    first_key, second_key = jax.random.split(jax.random.fold_in(key, 3))
    rough = jax.random.uniform(first_key, (TOKENS, CH), minval=0.5, maxval=2.0)
    spikes = jax.random.uniform(second_key, (TOKENS, 1), minval=0.5, maxval=1.0) * TOKENS
    return jnp.where(marked_rows[:, None], spikes, rough).astype(jnp.bfloat16)


def draw_ssm_a(key, part):
    keys = jax.random.split(jax.random.fold_in(key, 5), 3)
    slow_share = 0.5
    slow_flag = jax.random.bernoulli(keys[0], slow_share, (1, CH))
    slow_rate = jnp.exp(jax.random.uniform(keys[1], (NS, CH), minval=math.log(0.1), maxval=math.log(0.6))) / TOKENS
    fast_rate = jnp.exp(jax.random.uniform(keys[2], (NS, CH), minval=math.log(1.0 / TOKENS), maxval=math.log(1.0 / 30.0)))
    return (-jnp.where(slow_flag, slow_rate, fast_rate)).astype(jnp.float32)


def attention_pair(key):
    keys = jax.random.split(jax.random.fold_in(key, 11), 2)
    queries = jnp.clip(jax.random.normal(keys[0], (TOKENS, HQ * HEAD_SIZE)), -6.0, 6.0)
    stacked = jnp.clip(jax.random.normal(keys[1], (TOKENS, 2 * HK * HEAD_SIZE)), -6.0, 6.0)
    return (queries, stacked)


def draw_attn_q(key, part):
    return attention_pair(key)[0].astype(jnp.bfloat16)


def draw_attn_kv(key, part):
    return attention_pair(key)[1].astype(jnp.bfloat16)


def block_scale(stream_key, dims, pieces, least, high):
    def one(axis_at, shards_of):
        heights = jax.random.uniform(jax.random.fold_in(jax.random.fold_in(stream_key, 6), axis_at), (shards_of,), jnp.float32, least / len(pieces), high / len(pieces))
        return jnp.repeat(jnp.exp(heights), dims[axis_at] // shards_of).reshape((-1,) + (1,) * (len(dims) - axis_at - 1))

    gain = one(*pieces[0])
    for cut in pieces[1:]:
        gain = gain * one(*cut)
    return gain


def routed_block(rng, own, number, rows, count, top, reach, skew):
    order = jax.random.permutation(rng, count)
    packed, usual = load_shares(count, rows * top, reach, skew, True), load_shares(count, rows * top, reach, skew, False)
    places = jnp.arange(count)

    def named(lengths, offset_by):
        used = int((lengths > 0).sum())
        fixed = max(1, used // 4)
        moved = fixed + (places - fixed + offset_by * (used - fixed)) % max(1, count - fixed)
        return jnp.zeros((count,), jnp.int32).at[order[jnp.where(places < fixed, places, moved)]].set(jnp.asarray(lengths, jnp.int32))

    lengths = jnp.where(number % 4 == 0, named(packed, number // 4), named(usual, number - number // 4 - 1))
    mixed = jax.random.permutation(jax.random.fold_in(own, 3), count)
    giver, taker = mixed[0:count // 2 * 2:2], mixed[1:count // 2 * 2:2]
    margin = jnp.minimum(lengths[giver] - 1, reach - lengths[taker]) // 2
    margin = jnp.where((giver == order[0]) | (taker == order[0]) | (lengths[taker] == 0), 0, jnp.maximum(margin, 0))
    moved = jax.random.randint(jax.random.fold_in(own, 4), (count // 2,), 0, 1 << 20) % (margin + 1)
    lengths = lengths.at[giver].add(-moved).at[taker].add(moved)
    items = jnp.searchsorted(jnp.cumsum(lengths), jnp.arange(rows * top), side="right").astype(jnp.int32)
    table = items.reshape(top, rows).T
    table = table[jax.random.permutation(jax.random.fold_in(own, 1), rows)]
    offset_by = jax.random.randint(jax.random.fold_in(own, 2), (rows, 1), 0, top)
    return jnp.take_along_axis(table, (jnp.arange(top)[None, :] + offset_by) % top, axis=1)


def load_shares(amount, total, bound, slope, full):
    portions = [(1 << 20) // math.isqrt(rank ** slope) + 1 for rank in range(1, amount + 1)]
    largest = bound if full else min(bound, max(-(-total // amount), total * portions[0] // sum(portions)))
    least = 1 if total - largest >= amount - 1 else 0
    counts, spare = [largest] + [least] * (amount - 1), total - largest - least * (amount - 1)
    while spare > 0:
        free = [i for i in range(1, amount) if counts[i] < largest] or [i for i in range(1, amount) if counts[i] < bound]
        pool, left = sum([portions[i] for i in free]), spare
        for i in free:
            addition = min(bound - counts[i], max(1, left * portions[i] // pool), spare)
            counts[i] = counts[i] + addition
            spare = spare - addition
    return np.array(counts)


def normal_values(rng, shape, width, reach, cuts=(), held_as=jnp.bfloat16):
    array = width * jax.random.normal(rng, shape, jnp.float32)
    if cuts:
        array = array * block_scale(rng, shape, cuts, -0.22, 0.18)
    return jnp.clip(array, -reach, reach).astype(held_as)


def setup_inputs(seed: int = 0, part: int = 0) -> dict:
    splits = jax.random.split(jax.random.key(seed), 14)
    part_keys = jax.random.split(jax.random.fold_in(splits[13], part), 14)
    ssm_in = draw_ssm_in(jax.random.fold_in(jax.random.fold_in(splits[13], part), 71), part)
    ssm_dt = draw_ssm_dt(jax.random.fold_in(jax.random.fold_in(splits[13], part), 71), part)
    ssm_a = draw_ssm_a(jax.random.fold_in(splits[13], 71), part)
    ssm_b = normal_values(part_keys[3], (NS, TOKENS), (TOKENS ** -0.5), 0.1875, ((1, 16),), jnp.float32)
    ssm_c = normal_values(part_keys[4], (NS, TOKENS), (NS ** -0.5), 1.5, ((1, 16),), jnp.float32)
    attn_q = draw_attn_q(jax.random.fold_in(jax.random.fold_in(splits[13], part), 71), part)
    attn_kv = draw_attn_kv(jax.random.fold_in(jax.random.fold_in(splits[13], part), 71), part)
    moe_in = normal_values(part_keys[7], (TOKENS, D), 1.0, 6.0, ((0, 16),))
    moe_routes_keys = jax.random.split(jax.random.fold_in(part_keys[8], 1), TOKENS // TOK_DEV)
    moe_routes_turns = jax.random.permutation(jax.random.fold_in(part_keys[8], 3), TOKENS // TOK_DEV)
    moe_routes = jax.vmap(lambda own, number: routed_block(jax.random.fold_in(part_keys[8], 2), own, number, TOK_DEV, EXPERTS, 2, CAP, 1))(moe_routes_keys, moe_routes_turns).reshape((TOKENS, 2))
    moe_prob = jnp.clip(0.2 + 0.8 * jax.random.uniform(part_keys[9], (TOKENS, 2), jnp.float32) ** block_scale(part_keys[9], (TOKENS, 2), ((0, 16),), -0.2, 0.2), 0.2, 1.0)
    w_gate = normal_values(splits[10], (D, EXP_WIN * FF_EXP), D ** -0.5, 0.09375, ((1, 16),))
    w_up = normal_values(splits[11], (D, EXP_WIN * FF_EXP), D ** -0.5, 0.09375, ((1, 16),))
    w_down = normal_values(splits[12], (EXP_WIN * FF_EXP, D), FF_EXP ** -0.5, 0.1875, ((0, 16),))
    return dict(ssm_in=ssm_in, ssm_dt=ssm_dt, ssm_a=ssm_a, ssm_b=ssm_b, ssm_c=ssm_c, attn_q=attn_q, attn_kv=attn_kv, moe_in=moe_in, moe_routes=moe_routes, moe_prob=moe_prob, w_gate=w_gate, w_up=w_up, w_down=w_down)


def sweep(initial, values, deltas, rates, inject_rows, read_rows):

    def advance(carried, packet):
        value_row, delta_row, inject_row, read_row = packet
        carried = jnp.exp(delta_row[None, :] * rates) * carried + (delta_row * value_row)[None, :] * inject_row[:, None]
        return (carried, lax.optimization_barrier(jnp.sum(read_row[:, None] * carried, axis=0)))
    return lax.scan(advance, initial, (values, deltas, inject_rows.T, read_rows.T), unroll=8)

def attend(queries, window, query_pos, key_pos):
    count = queries.shape[0]
    key_count = window.shape[0]
    repeat = HQ // HK
    query_head_tensor = queries.reshape(count, HK, repeat, HEAD_SIZE).astype(jnp.float32)
    key_head_tensor = window[:, :HK * HEAD_SIZE].reshape(key_count, HK, HEAD_SIZE).astype(jnp.float32)
    value_head_tensor = window[:, HK * HEAD_SIZE:].reshape(key_count, HK, HEAD_SIZE).astype(jnp.float32)
    attention_scores = jnp.einsum('bajq,oaq->ajbo', query_head_tensor, key_head_tensor) / math.sqrt(HEAD_SIZE)
    allowed = (key_pos[None, :] >= 0) & (key_pos[None, :] <= query_pos[:, None])
    attention_scores = jnp.where(allowed[None, None], attention_scores, -jnp.inf)
    row_max = lax.optimization_barrier(jnp.max(attention_scores, axis=-1, keepdims=True))
    expd = jnp.exp(attention_scores - row_max)
    probabilities = (expd / lax.optimization_barrier(jnp.sum(expd, axis=-1, keepdims=True))).astype(jnp.bfloat16)
    probabilities = lax.optimization_barrier(probabilities).astype(jnp.float32)
    expert_mixture = jnp.einsum('kyje,eku->jkyu', probabilities, value_head_tensor)
    return expert_mixture.reshape(count, HQ * HEAD_SIZE).astype(jnp.bfloat16)

def reference(ssm_in, ssm_dt, ssm_a, ssm_b, ssm_c, attn_q, attn_kv, moe_in, moe_routes, moe_prob, w_gate, w_up, w_down):
    values = ssm_in.astype(jnp.float32)
    deltas = ssm_dt.astype(jnp.float32)
    initial = jnp.zeros((NS, CH), jnp.float32)
    final_state, reads = sweep(initial, values, deltas, ssm_a, ssm_b, ssm_c)
    ssm_out = reads.astype(jnp.bfloat16)
    padded = jnp.concatenate([jnp.zeros((2 * TOK_DEV, 2 * HK * HEAD_SIZE), jnp.bfloat16), attn_kv], axis=0)

    def one_block(block_index):
        first_row = block_index * TOK_DEV
        queries = lax.dynamic_slice_in_dim(attn_q, first_row, TOK_DEV, 0)
        window = lax.dynamic_slice_in_dim(padded, first_row, 3 * TOK_DEV, 0)
        query_pos = first_row + jnp.arange(TOK_DEV, dtype=jnp.int32)
        key_pos = first_row - 2 * TOK_DEV + jnp.arange(3 * TOK_DEV, dtype=jnp.int32)
        return attend(queries, window, query_pos, key_pos)
    attn_out = lax.map(one_block, jnp.arange(N_SEQ, dtype=jnp.int32)).reshape(TOKENS, HQ * HEAD_SIZE)
    stream = (moe_in.astype(jnp.float32) + ssm_out.astype(jnp.float32) + attn_out.astype(jnp.float32)).astype(jnp.bfloat16)
    slots_total = N_SEQ * CAP
    expert_ids = jnp.arange(EXP_WIN, dtype=jnp.int32)
    matches = moe_routes[:, :, None] == expert_ids[None, None, :]
    routed = jnp.any(matches, axis=1).astype(jnp.int32)
    route_share = lax.optimization_barrier(jnp.sum(jnp.where(matches, moe_prob[:, :, None], 0.0), axis=1))
    position_rank = jnp.cumsum(routed.reshape(N_SEQ, TOK_DEV, EXP_WIN), axis=1).reshape(TOKENS, EXP_WIN) - 1
    block_of = jnp.arange(TOKENS, dtype=jnp.int32) // TOK_DEV
    slot_index = jnp.where(routed == 1, block_of[:, None] * CAP + position_rank, slots_total).astype(jnp.int32)
    padded_in = jnp.concatenate([stream, jnp.zeros((1, D), jnp.bfloat16)], axis=0)
    combined = jnp.zeros((TOKENS, D), jnp.float32)
    for expert in range(EXP_WIN):
        owners = jnp.full((slots_total + 1,), TOKENS, jnp.int32)
        owners = owners.at[slot_index[:, expert]].set(jnp.arange(TOKENS, dtype=jnp.int32))[:slots_total]
        gathered = padded_in[owners]
        low = expert * FF_EXP
        gate_pre = jnp.dot(gathered, w_gate[:, low:low + FF_EXP], preferred_element_type=jnp.float32)
        up_pre = jnp.dot(gathered, w_up[:, low:low + FF_EXP], preferred_element_type=jnp.float32)
        hidden_act = (jax.nn.silu(gate_pre) * up_pre).astype(jnp.bfloat16)
        result = jnp.zeros((slots_total, D), jnp.float32)
        for block_index in range(GROUP):
            start = block_index * FF_DEV
            partial_value = jnp.dot(hidden_act[:, start:start + FF_DEV], w_down[low + start:low + start + FF_DEV, :], preferred_element_type=jnp.float32).astype(jnp.bfloat16)
            result = result + lax.optimization_barrier(partial_value).astype(jnp.float32)
        result_pad = jnp.concatenate([result, jnp.zeros((1, D), jnp.float32)], axis=0)
        combined = combined + route_share[:, expert:expert + 1] * result_pad[slot_index[:, expert]]
    moe_out = combined.astype(jnp.bfloat16)
    return (ssm_out, attn_out, moe_out)
```

```python
import math

import jax
import jax.numpy as jnp
from jax import lax
from jax.sharding import PartitionSpec as P

HQ = 32
HK = 8
HEAD_SIZE = 128
EXP_WIN = 4
CAP = 12


def prefix(value, axis, join, neutral):
    count, mine = (lax.axis_size(axis), lax.axis_index(axis))
    pieces = jax.tree.map(lambda part: lax.all_gather(part, axis), value)
    running = jax.tree.map(
        lambda part, zero: jnp.full_like(part, 0) + jnp.asarray(zero, part.dtype), value, neutral
    )

    def hop(position, running):
        longer = join(running, jax.tree.map(lambda part: part[position], pieces))
        return jax.tree.map(lambda new, old: jnp.where(position < mine, new, old), longer, running)

    return lax.fori_loop(0, count - 1, hop, running)


def shifted(value, axis, by):
    devices = lax.axis_size(axis)
    pairs = [(i, i + by) for i in range(devices) if 0 <= i + by < devices]
    return lax.ppermute(value, axis, pairs)


def sweep(initial, values, deltas, rates, inject_rows, read_rows):

    def advance(carried, packet):
        value_row, delta_row, inject_row, read_row = packet
        carried = (
            jnp.exp(delta_row[None, :] * rates) * carried
            + (delta_row * value_row)[None, :] * inject_row[:, None]
        )
        return (carried, jnp.sum(read_row[:, None] * carried, axis=0))

    return lax.scan(advance, initial, (values, deltas, inject_rows.T, read_rows.T), unroll=8)


def ssm_correct(local_read, local_end, deltas, rates, read_rows):
    mine = lax.axis_index("seq")
    running = jnp.cumsum(deltas, axis=0)
    ends = lax.all_gather(local_end, "seq")
    sums = lax.all_gather(running[-1], "seq")
    devices = sums.shape[0]
    order = jnp.arange(devices, dtype=jnp.int32)
    masked = jnp.where((order < mine)[:, None], sums, 0.0)
    after = jnp.sum(masked, axis=0)[None, :] - jnp.cumsum(masked, axis=0)
    after = jnp.maximum(after, 0.0)
    carry = jnp.exp(rates[None] * after[:, None, :]) * ends
    incoming = jnp.sum(jnp.where((order < mine)[:, None, None], carry, 0.0), axis=0)
    growth = jnp.exp(rates[None] * running[:, None, :]) * incoming[None]
    fix = jnp.sum(read_rows.T[:, :, None] * growth, axis=1)
    return (local_read + fix).astype(jnp.bfloat16)


def chain_join(earlier, later):
    return (earlier[0] * later[0], later[0] * earlier[1] + later[1])


def attend(queries, window, query_pos, key_pos):
    count = queries.shape[0]
    key_count = window.shape[0]
    repeat = HQ // HK
    query_head_tensor = queries.reshape(count, HK, repeat, HEAD_SIZE)
    key_head_tensor = window[:, : HK * HEAD_SIZE].reshape(key_count, HK, HEAD_SIZE)
    value_head_tensor = window[:, HK * HEAD_SIZE :].reshape(key_count, HK, HEAD_SIZE)
    attention_scores = jnp.einsum(
        "bajq,oaq->ajbo", query_head_tensor, key_head_tensor, preferred_element_type=jnp.float32
    ) / math.sqrt(HEAD_SIZE)
    allowed = (key_pos[None, :] >= 0) & (key_pos[None, :] <= query_pos[:, None])
    attention_scores = jnp.where(allowed[None, None], attention_scores, -jnp.inf)
    row_max = jnp.max(attention_scores, axis=-1, keepdims=True)
    expd = jnp.exp(attention_scores - row_max)
    probabilities = (expd / jnp.sum(expd, axis=-1, keepdims=True)).astype(jnp.bfloat16)
    expert_mixture = jnp.einsum(
        "kyje,eku->jkyu", probabilities, value_head_tensor, preferred_element_type=jnp.float32
    )
    return expert_mixture.reshape(count, HQ * HEAD_SIZE).astype(jnp.bfloat16)


def expert_partial(gathered, w_gate, w_up, w_down):
    gate_pre = jnp.dot(gathered, w_gate, preferred_element_type=jnp.float32)
    up_pre = jnp.dot(gathered, w_up, preferred_element_type=jnp.float32)
    hidden_act = (jax.nn.silu(gate_pre) * up_pre).astype(jnp.bfloat16)
    return jnp.dot(hidden_act, w_down, preferred_element_type=jnp.float32).astype(jnp.bfloat16)


def body(
    ssm_in,
    ssm_dt,
    ssm_a,
    ssm_b,
    ssm_c,
    attn_q,
    attn_kv,
    moe_in,
    moe_routes,
    moe_prob,
    w_gate,
    w_up,
    w_down,
):
    values = ssm_in.astype(jnp.float32)
    deltas = ssm_dt.astype(jnp.float32)
    initial = jnp.zeros(ssm_a.shape, jnp.float32)
    local_end, local_read = sweep(initial, values, deltas, ssm_a, ssm_b, ssm_c)
    ssm_out = ssm_correct(local_read, local_end, deltas, ssm_a, ssm_c)
    count = attn_q.shape[0]
    block_index = lax.axis_index("seq")
    one_back = shifted(attn_kv, "seq", 1)
    two_back = shifted(attn_kv, "seq", 2)
    window = jnp.concatenate([two_back, one_back, attn_kv], axis=0)
    first_row = block_index * count
    query_pos = first_row + jnp.arange(count, dtype=jnp.int32)
    key_pos = first_row - 2 * count + jnp.arange(3 * count, dtype=jnp.int32)
    attn_out = attend(attn_q, window, query_pos, key_pos)
    stream = (
        moe_in.astype(jnp.float32) + ssm_out.astype(jnp.float32) + attn_out.astype(jnp.float32)
    ).astype(jnp.bfloat16)
    local_tokens = stream.shape[0]
    width = stream.shape[1]
    seq_count = lax.axis_size("seq")
    group = seq_count // EXP_WIN
    expert_ids = jnp.arange(EXP_WIN, dtype=jnp.int32)
    matches = moe_routes[:, :, None] == expert_ids[None, None, :]
    routed = jnp.any(matches, axis=1).astype(jnp.int32)
    route_share = jnp.sum(jnp.where(matches, moe_prob[:, :, None], 0.0), axis=1)
    position_rank = jnp.cumsum(routed, axis=0) - 1
    picker = (routed[:, :, None] == 1) & (
        position_rank[:, :, None] == jnp.arange(CAP, dtype=jnp.int32)[None, None, :]
    )
    packed = jnp.einsum(
        "tek,td->ekd", picker.astype(jnp.bfloat16), stream, preferred_element_type=jnp.float32
    ).astype(jnp.bfloat16)
    outgoing = jnp.repeat(packed, group, axis=0)
    arrived = lax.all_to_all(outgoing, "seq", split_axis=0, concat_axis=0, tiled=True)
    gathered = arrived.reshape(-1, arrived.shape[-1])
    partial_value = expert_partial(gathered, w_gate, w_up, w_down)
    returned = lax.all_to_all(
        partial_value.reshape(arrived.shape), "seq", split_axis=0, concat_axis=0, tiled=True
    )
    summed = jnp.sum(returned.reshape(EXP_WIN, group, CAP, width), axis=1, dtype=jnp.float32)
    weighting = (picker.astype(jnp.float32) * route_share[:, :, None]).reshape(
        local_tokens, EXP_WIN * CAP
    )
    combined = jnp.dot(
        weighting,
        summed.reshape(EXP_WIN * CAP, width),
        precision=lax.Precision.HIGHEST,
        preferred_element_type=jnp.float32,
    )
    moe_out = combined.astype(jnp.bfloat16)
    return (ssm_out, attn_out, moe_out)


def solution(mesh):
    return jax.shard_map(
        body,
        mesh=mesh,
        in_specs=(
            P(("grp", "seq"), None),
            P(("grp", "seq"), None),
            P(),
            P(None, ("grp", "seq")),
            P(None, ("grp", "seq")),
            P(("grp", "seq"), None),
            P(("grp", "seq"), None),
            P(("grp", "seq"), None),
            P(("grp", "seq"), None),
            P(("grp", "seq"), None),
            P(None, "seq"),
            P(None, "seq"),
            P("seq", None),
        ),
        out_specs=(P(("grp", "seq"), None), P(("grp", "seq"), None), P(("grp", "seq"), None)),
        check_vma=False,
    )
```

```python
import functools
import math

import jax
import jax.numpy as jnp
from jax import lax
from jax.sharding import Mesh, PartitionSpec as P

HQ = 32
HK = 8
HEAD_SIZE = 128
EXP_WIN = 4
CAP = 12
SEQ = ("eg", "kg")


def shifted(value, axis, by, devices):
    pairs = [(i, i + by) for i in range(devices) if 0 <= i + by < devices]
    return lax.ppermute(value, axis, pairs)


def sweep(initial, values, deltas, rates, inject_rows, read_rows):

    def advance(carried, packet):
        value_row, delta_row, inject_row, read_row = packet
        carried = (
            jnp.exp(delta_row[None, :] * rates) * carried
            + (delta_row * value_row)[None, :] * inject_row[:, None]
        )
        return (carried, jnp.sum(read_row[:, None] * carried, axis=0))

    return lax.scan(advance, initial, (values, deltas, inject_rows.T, read_rows.T), unroll=8)


def ssm_correct(local_read, local_end, deltas, rates, read_rows):
    mine = lax.axis_index(SEQ)
    running = jnp.cumsum(deltas, axis=0)
    both = lax.all_gather(jnp.concatenate([local_end, running[-1:]], axis=0), SEQ)
    ends = both[:, :-1]
    sums = both[:, -1]
    devices = sums.shape[0]
    order = jnp.arange(devices, dtype=jnp.int32)
    masked = jnp.where((order < mine)[:, None], sums, 0.0)
    after = jnp.sum(masked, axis=0)[None, :] - jnp.cumsum(masked, axis=0)
    after = jnp.maximum(after, 0.0)
    carry = jnp.exp(rates[None] * after[:, None, :]) * ends
    incoming = jnp.sum(jnp.where((order < mine)[:, None, None], carry, 0.0), axis=0)
    growth = jnp.exp(rates[None] * running[:, None, :]) * incoming[None]
    fix = jnp.sum(read_rows.T[:, :, None] * growth, axis=1)
    return (local_read + fix).astype(jnp.bfloat16)


def attend(queries, window, query_pos, key_pos):
    count = queries.shape[0]
    key_count = window.shape[0]
    repeat = HQ // HK
    query_head_tensor = queries.reshape(count, HK, repeat, HEAD_SIZE)
    key_head_tensor = window[:, : HK * HEAD_SIZE].reshape(key_count, HK, HEAD_SIZE)
    value_head_tensor = window[:, HK * HEAD_SIZE :].reshape(key_count, HK, HEAD_SIZE)
    attention_scores = jnp.einsum(
        "bajq,oaq->ajbo", query_head_tensor, key_head_tensor, preferred_element_type=jnp.float32
    ) / math.sqrt(HEAD_SIZE)
    allowed = (key_pos[None, :] >= 0) & (key_pos[None, :] <= query_pos[:, None])
    attention_scores = jnp.where(allowed[None, None], attention_scores, -jnp.inf)
    row_max = jnp.max(attention_scores, axis=-1, keepdims=True)
    expd = jnp.exp(attention_scores - row_max)
    probabilities = (expd / jnp.sum(expd, axis=-1, keepdims=True)).astype(jnp.bfloat16)
    expert_mixture = jnp.einsum(
        "kyje,eku->jkyu", probabilities, value_head_tensor, preferred_element_type=jnp.float32
    )
    return expert_mixture.reshape(count, HQ * HEAD_SIZE).astype(jnp.bfloat16)


def expert_partial(gathered, w_gate, w_up, w_down):
    gate_pre = jnp.dot(gathered, w_gate, preferred_element_type=jnp.float32)
    up_pre = jnp.dot(gathered, w_up, preferred_element_type=jnp.float32)
    hidden_act = (jax.nn.silu(gate_pre) * up_pre).astype(jnp.bfloat16)
    return jnp.dot(hidden_act, w_down, preferred_element_type=jnp.float32).astype(jnp.bfloat16)


def body(
    ssm_in,
    ssm_dt,
    ssm_a,
    ssm_b,
    ssm_c,
    attn_q,
    attn_kv,
    moe_in,
    moe_routes,
    moe_prob,
    w_gate,
    w_up,
    w_down,
    *,
    seq_count,
):
    values = ssm_in.astype(jnp.float32)
    deltas = ssm_dt.astype(jnp.float32)
    initial = jnp.zeros(ssm_a.shape, jnp.float32)
    local_end, local_read = sweep(initial, values, deltas, ssm_a, ssm_b, ssm_c)
    ssm_out = ssm_correct(local_read, local_end, deltas, ssm_a, ssm_c)
    count = attn_q.shape[0]
    block_index = lax.axis_index(SEQ)
    one_back = shifted(attn_kv, SEQ, 1, seq_count)
    two_back = shifted(attn_kv, SEQ, 2, seq_count)
    window = jnp.concatenate([two_back, one_back, attn_kv], axis=0)
    first_row = block_index * count
    query_pos = first_row + jnp.arange(count, dtype=jnp.int32)
    key_pos = first_row - 2 * count + jnp.arange(3 * count, dtype=jnp.int32)
    attn_out = attend(attn_q, window, query_pos, key_pos)
    stream = (
        moe_in.astype(jnp.float32) + ssm_out.astype(jnp.float32) + attn_out.astype(jnp.float32)
    ).astype(jnp.bfloat16)
    local_tokens = stream.shape[0]
    width = stream.shape[1]
    expert_ids = jnp.arange(EXP_WIN, dtype=jnp.int32)
    matches = moe_routes[:, :, None] == expert_ids[None, None, :]
    routed = jnp.any(matches, axis=1).astype(jnp.int32)
    route_share = jnp.sum(jnp.where(matches, moe_prob[:, :, None], 0.0), axis=1)
    position_rank = jnp.cumsum(routed, axis=0) - 1
    picker = (routed[:, :, None] == 1) & (
        position_rank[:, :, None] == jnp.arange(CAP, dtype=jnp.int32)[None, None, :]
    )
    packed = jnp.einsum(
        "tek,td->ekd", picker.astype(jnp.bfloat16), stream, preferred_element_type=jnp.float32
    ).astype(jnp.bfloat16)
    own = lax.axis_index("eg")
    pieces = [lax.dynamic_index_in_dim(packed, own, 0, keepdims=False)]
    for by in range(1, EXP_WIN):
        piece = lax.dynamic_index_in_dim(packed, (own + by) % EXP_WIN, 0, keepdims=False)
        pairs = [(i, (i + by) % EXP_WIN) for i in range(EXP_WIN)]
        pieces.append(lax.ppermute(piece, "eg", pairs))
    local_block = jnp.stack(pieces)
    arrived = lax.all_gather(local_block, "kg")
    gathered = arrived.reshape(-1, width)
    partial_value = expert_partial(gathered, w_gate, w_up, w_down)
    reduced = lax.psum_scatter(
        partial_value.reshape(arrived.shape).astype(jnp.float32), "kg", scatter_dimension=0, tiled=True
    )[0]
    back = [reduced[0]]
    for by in range(1, EXP_WIN):
        pairs = [(i, (i - by) % EXP_WIN) for i in range(EXP_WIN)]
        back.append(lax.ppermute(reduced[by], "eg", pairs))
    summed = jnp.stack(back)
    turn = (own + jnp.arange(EXP_WIN, dtype=jnp.int32)) % EXP_WIN
    weighting = (picker.astype(jnp.float32) * route_share[:, :, None])[:, turn, :].reshape(
        local_tokens, EXP_WIN * CAP
    )
    combined = jnp.dot(
        weighting,
        summed.reshape(EXP_WIN * CAP, width),
        precision=lax.Precision.HIGHEST,
        preferred_element_type=jnp.float32,
    )
    moe_out = combined.astype(jnp.bfloat16)
    return (ssm_out, attn_out, moe_out)


def solution(mesh):
    groups = mesh.shape["grp"]
    seq_count = mesh.shape["seq"]
    fine = Mesh(
        mesh.devices.reshape(groups, EXP_WIN, seq_count // EXP_WIN), ("grp", "eg", "kg")
    )
    rows = P(("grp",) + SEQ, None)
    return jax.shard_map(
        functools.partial(body, seq_count=seq_count),
        mesh=fine,
        in_specs=(
            rows,
            rows,
            P(),
            P(None, ("grp",) + SEQ),
            P(None, ("grp",) + SEQ),
            rows,
            rows,
            rows,
            rows,
            rows,
            P(None, SEQ),
            P(None, SEQ),
            P(SEQ, None),
        ),
        out_specs=(rows, rows, rows),
        check_vma=False,
    )
```

```python
import math

import jax
import jax.numpy as jnp
from jax import lax
from jax.experimental import pallas as pl
from jax.experimental.pallas import tpu as pltpu
from jax.sharding import PartitionSpec as P

HQ = 32
HK = 8
HEAD_SIZE = 128
EXP_WIN = 4
CAP = 12


def shifted(value, axis, by):
    devices = lax.axis_size(axis)
    pairs = [(i, i + by) for i in range(devices) if 0 <= i + by < devices]
    return lax.ppermute(value, axis, pairs)


def scan_kernel(b_ref, c_ref, dt_ref, inj_ref, a_ref, read_ref, end_ref):
    states = a_ref.shape[0]
    steps = dt_ref.shape[0]
    h = [jnp.zeros(dt_ref.shape[1:], jnp.float32) for _ in range(states)]
    for t in range(steps):
        d = dt_ref[t]
        u = inj_ref[t]
        total = None
        for n in range(states):
            h[n] = jnp.exp(d * a_ref[n]) * h[n] + b_ref[n, t] * u
            term = c_ref[n, t] * h[n]
            total = term if total is None else total + term
        read_ref[t] = total
    for n in range(states):
        end_ref[n] = h[n]


def sweep(values, deltas, rates, inject_rows, read_rows):
    steps, channels = deltas.shape
    states = rates.shape[0]
    lanes = 128
    rows = channels // lanes
    tile = 8
    dt3 = deltas.reshape(steps, rows, lanes)
    inj3 = (deltas * values).reshape(steps, rows, lanes)
    a3 = rates.reshape(states, rows, lanes)
    read3, end3 = pl.pallas_call(
        scan_kernel,
        grid=(rows // tile,),
        in_specs=[
            pl.BlockSpec(memory_space=pltpu.SMEM),
            pl.BlockSpec(memory_space=pltpu.SMEM),
            pl.BlockSpec((steps, tile, lanes), lambda j: (0, j, 0)),
            pl.BlockSpec((steps, tile, lanes), lambda j: (0, j, 0)),
            pl.BlockSpec((states, tile, lanes), lambda j: (0, j, 0)),
        ],
        out_specs=[
            pl.BlockSpec((steps, tile, lanes), lambda j: (0, j, 0)),
            pl.BlockSpec((states, tile, lanes), lambda j: (0, j, 0)),
        ],
        out_shape=[
            jax.ShapeDtypeStruct((steps, rows, lanes), jnp.float32),
            jax.ShapeDtypeStruct((states, rows, lanes), jnp.float32),
        ],
    )(inject_rows, read_rows, dt3, inj3, a3)
    return end3.reshape(states, channels), read3.reshape(steps, channels)


def ssm_correct(local_read, local_end, deltas, rates, read_rows):
    mine = lax.axis_index("seq")
    running = jnp.cumsum(deltas, axis=0)
    ends = lax.all_gather(local_end, "seq")
    sums = lax.all_gather(running[-1], "seq")
    devices = sums.shape[0]
    order = jnp.arange(devices, dtype=jnp.int32)
    masked = jnp.where((order < mine)[:, None], sums, 0.0)
    after = jnp.sum(masked, axis=0)[None, :] - jnp.cumsum(masked, axis=0)
    after = jnp.maximum(after, 0.0)
    carry = jnp.exp(rates[None] * after[:, None, :]) * ends
    incoming = jnp.sum(jnp.where((order < mine)[:, None, None], carry, 0.0), axis=0)
    growth = jnp.exp(rates[None] * running[:, None, :]) * incoming[None]
    fix = jnp.sum(read_rows.T[:, :, None] * growth, axis=1)
    return (local_read + fix).astype(jnp.bfloat16)


def attend(queries, window, query_pos, key_pos):
    count = queries.shape[0]
    key_count = window.shape[0]
    repeat = HQ // HK
    query_head_tensor = queries.reshape(count, HK, repeat, HEAD_SIZE)
    key_head_tensor = window[:, : HK * HEAD_SIZE].reshape(key_count, HK, HEAD_SIZE)
    value_head_tensor = window[:, HK * HEAD_SIZE :].reshape(key_count, HK, HEAD_SIZE)
    attention_scores = jnp.einsum(
        "bajq,oaq->ajbo", query_head_tensor, key_head_tensor, preferred_element_type=jnp.float32
    ) / math.sqrt(HEAD_SIZE)
    allowed = (key_pos[None, :] >= 0) & (key_pos[None, :] <= query_pos[:, None])
    attention_scores = jnp.where(allowed[None, None], attention_scores, -jnp.inf)
    row_max = jnp.max(attention_scores, axis=-1, keepdims=True)
    expd = jnp.exp(attention_scores - row_max)
    probabilities = (expd / jnp.sum(expd, axis=-1, keepdims=True)).astype(jnp.bfloat16)
    expert_mixture = jnp.einsum(
        "kyje,eku->jkyu", probabilities, value_head_tensor, preferred_element_type=jnp.float32
    )
    return expert_mixture.reshape(count, HQ * HEAD_SIZE).astype(jnp.bfloat16)


def expert_partial(gathered, w_gate, w_up, w_down):
    gate_pre = jnp.dot(gathered, w_gate, preferred_element_type=jnp.float32)
    up_pre = jnp.dot(gathered, w_up, preferred_element_type=jnp.float32)
    hidden_act = (jax.nn.silu(gate_pre) * up_pre).astype(jnp.bfloat16)
    return jnp.dot(hidden_act, w_down, preferred_element_type=jnp.float32).astype(jnp.bfloat16)


def body(
    ssm_in,
    ssm_dt,
    ssm_a,
    ssm_b,
    ssm_c,
    attn_q,
    attn_kv,
    moe_in,
    moe_routes,
    moe_prob,
    w_gate,
    w_up,
    w_down,
):
    values = ssm_in.astype(jnp.float32)
    deltas = ssm_dt.astype(jnp.float32)
    local_end, local_read = sweep(values, deltas, ssm_a, ssm_b, ssm_c)
    ssm_out = ssm_correct(local_read, local_end, deltas, ssm_a, ssm_c)
    count = attn_q.shape[0]
    block_index = lax.axis_index("seq")
    one_back = shifted(attn_kv, "seq", 1)
    two_back = shifted(attn_kv, "seq", 2)
    window = jnp.concatenate([two_back, one_back, attn_kv], axis=0)
    first_row = block_index * count
    query_pos = first_row + jnp.arange(count, dtype=jnp.int32)
    key_pos = first_row - 2 * count + jnp.arange(3 * count, dtype=jnp.int32)
    attn_out = attend(attn_q, window, query_pos, key_pos)
    stream = (
        moe_in.astype(jnp.float32) + ssm_out.astype(jnp.float32) + attn_out.astype(jnp.float32)
    ).astype(jnp.bfloat16)
    local_tokens = stream.shape[0]
    width = stream.shape[1]
    seq_count = lax.axis_size("seq")
    group = seq_count // EXP_WIN
    expert_ids = jnp.arange(EXP_WIN, dtype=jnp.int32)
    matches = moe_routes[:, :, None] == expert_ids[None, None, :]
    routed = jnp.any(matches, axis=1).astype(jnp.int32)
    route_share = jnp.sum(jnp.where(matches, moe_prob[:, :, None], 0.0), axis=1)
    position_rank = jnp.cumsum(routed, axis=0) - 1
    picker = (routed[:, :, None] == 1) & (
        position_rank[:, :, None] == jnp.arange(CAP, dtype=jnp.int32)[None, None, :]
    )
    packed = jnp.einsum(
        "tek,td->ekd", picker.astype(jnp.bfloat16), stream, preferred_element_type=jnp.float32
    ).astype(jnp.bfloat16)
    outgoing = jnp.repeat(packed, group, axis=0)
    arrived = lax.all_to_all(outgoing, "seq", split_axis=0, concat_axis=0, tiled=True)
    gathered = arrived.reshape(-1, arrived.shape[-1])
    partial_value = expert_partial(gathered, w_gate, w_up, w_down)
    returned = lax.all_to_all(
        partial_value.reshape(arrived.shape), "seq", split_axis=0, concat_axis=0, tiled=True
    )
    summed = jnp.sum(returned.reshape(EXP_WIN, group, CAP, width), axis=1, dtype=jnp.float32)
    weighting = (picker.astype(jnp.float32) * route_share[:, :, None]).reshape(
        local_tokens, EXP_WIN * CAP
    )
    combined = jnp.dot(
        weighting,
        summed.reshape(EXP_WIN * CAP, width),
        precision=lax.Precision.HIGHEST,
        preferred_element_type=jnp.float32,
    )
    moe_out = combined.astype(jnp.bfloat16)
    return (ssm_out, attn_out, moe_out)


def solution(mesh):
    return jax.shard_map(
        body,
        mesh=mesh,
        in_specs=(
            P(("grp", "seq"), None),
            P(("grp", "seq"), None),
            P(),
            P(None, ("grp", "seq")),
            P(None, ("grp", "seq")),
            P(("grp", "seq"), None),
            P(("grp", "seq"), None),
            P(("grp", "seq"), None),
            P(("grp", "seq"), None),
            P(("grp", "seq"), None),
            P(None, "seq"),
            P(None, "seq"),
            P("seq", None),
        ),
        out_specs=(P(("grp", "seq"), None), P(("grp", "seq"), None), P(("grp", "seq"), None)),
        check_vma=False,
    )
```

```python
import math

import jax
import jax.numpy as jnp
from jax import lax
from jax.experimental import pallas as pl
from jax.experimental.pallas import tpu as pltpu
from jax.sharding import PartitionSpec as P

HQ = 32
HK = 8
HEAD_SIZE = 128
EXP_WIN = 4
CAP = 12


def shifted(value, axis, by):
    devices = lax.axis_size(axis)
    pairs = [(i, i + by) for i in range(devices) if 0 <= i + by < devices]
    return lax.ppermute(value, axis, pairs)


def scan_kernel(b_ref, c_ref, dt_ref, inj_ref, a_ref, read_ref, end_ref):
    states = a_ref.shape[0]
    steps = dt_ref.shape[0]
    h = [jnp.zeros(dt_ref.shape[1:], jnp.float32) for _ in range(states)]
    for t in range(steps):
        d = dt_ref[t]
        u = inj_ref[t]
        total = None
        for n in range(states):
            h[n] = jnp.exp(d * a_ref[n]) * h[n] + b_ref[n, t] * u
            term = c_ref[n, t] * h[n]
            total = term if total is None else total + term
        read_ref[t] = total
    for n in range(states):
        end_ref[n] = h[n]


def sweep(values, deltas, rates, inject_rows, read_rows):
    steps, channels = deltas.shape
    states = rates.shape[0]
    lanes = 128
    rows = channels // lanes
    tile = 8
    dt3 = deltas.reshape(steps, rows, lanes)
    inj3 = (deltas * values).reshape(steps, rows, lanes)
    a3 = rates.reshape(states, rows, lanes)
    read3, end3 = pl.pallas_call(
        scan_kernel,
        grid=(rows // tile,),
        in_specs=[
            pl.BlockSpec(memory_space=pltpu.SMEM),
            pl.BlockSpec(memory_space=pltpu.SMEM),
            pl.BlockSpec((steps, tile, lanes), lambda j: (0, j, 0)),
            pl.BlockSpec((steps, tile, lanes), lambda j: (0, j, 0)),
            pl.BlockSpec((states, tile, lanes), lambda j: (0, j, 0)),
        ],
        out_specs=[
            pl.BlockSpec((steps, tile, lanes), lambda j: (0, j, 0)),
            pl.BlockSpec((states, tile, lanes), lambda j: (0, j, 0)),
        ],
        out_shape=[
            jax.ShapeDtypeStruct((steps, rows, lanes), jnp.float32),
            jax.ShapeDtypeStruct((states, rows, lanes), jnp.float32),
        ],
    )(inject_rows, read_rows, dt3, inj3, a3)
    return end3.reshape(states, channels), read3.reshape(steps, channels)


def ssm_correct(local_read, local_end, deltas, rates, read_rows):
    mine = lax.axis_index("seq")
    running = jnp.cumsum(deltas, axis=0)
    ends = lax.all_gather(local_end, "seq")
    sums = lax.optimization_barrier(lax.all_gather(running[-8:], "seq"))[:, -1]
    devices = sums.shape[0]
    order = jnp.arange(devices, dtype=jnp.int32)
    masked = jnp.where((order < mine)[:, None], sums, 0.0)
    after = jnp.sum(masked, axis=0)[None, :] - jnp.cumsum(masked, axis=0)
    after = jnp.maximum(after, 0.0)
    carry = jnp.exp(rates[None] * after[:, None, :]) * ends
    incoming = jnp.sum(jnp.where((order < mine)[:, None, None], carry, 0.0), axis=0)
    growth = jnp.exp(rates[None] * running[:, None, :]) * incoming[None]
    fix = jnp.sum(read_rows.T[:, :, None] * growth, axis=1)
    return (local_read + fix).astype(jnp.bfloat16)


def attend(queries, window, query_pos, key_pos):
    count = queries.shape[0]
    key_count = window.shape[0]
    repeat = HQ // HK
    query_head_tensor = queries.reshape(count, HK, repeat, HEAD_SIZE)
    key_head_tensor = window[:, : HK * HEAD_SIZE].reshape(key_count, HK, HEAD_SIZE)
    value_head_tensor = window[:, HK * HEAD_SIZE :].reshape(key_count, HK, HEAD_SIZE)
    attention_scores = jnp.einsum(
        "bajq,oaq->ajbo", query_head_tensor, key_head_tensor, preferred_element_type=jnp.float32
    ) / math.sqrt(HEAD_SIZE)
    allowed = (key_pos[None, :] >= 0) & (key_pos[None, :] <= query_pos[:, None])
    attention_scores = jnp.where(allowed[None, None], attention_scores, -jnp.inf)
    row_max = jnp.max(attention_scores, axis=-1, keepdims=True)
    expd = jnp.exp(attention_scores - row_max)
    probabilities = (expd / jnp.sum(expd, axis=-1, keepdims=True)).astype(jnp.bfloat16)
    expert_mixture = jnp.einsum(
        "kyje,eku->jkyu", probabilities, value_head_tensor, preferred_element_type=jnp.float32
    )
    return expert_mixture.reshape(count, HQ * HEAD_SIZE).astype(jnp.bfloat16)


def expert_partial(gathered, w_gate, w_up, w_down):
    gate_pre = jnp.dot(gathered, w_gate, preferred_element_type=jnp.float32)
    up_pre = jnp.dot(gathered, w_up, preferred_element_type=jnp.float32)
    hidden_act = (jax.nn.silu(gate_pre) * up_pre).astype(jnp.bfloat16)
    return jnp.dot(hidden_act, w_down, preferred_element_type=jnp.float32).astype(jnp.bfloat16)


def body(
    ssm_in,
    ssm_dt,
    ssm_a,
    ssm_b,
    ssm_c,
    attn_q,
    attn_kv,
    moe_in,
    moe_routes,
    moe_prob,
    w_gate,
    w_up,
    w_down,
):
    values = ssm_in.astype(jnp.float32)
    deltas = ssm_dt.astype(jnp.float32)
    local_end, local_read = sweep(values, deltas, ssm_a, ssm_b, ssm_c)
    ssm_out = ssm_correct(local_read, local_end, deltas, ssm_a, ssm_c)
    count = attn_q.shape[0]
    block_index = lax.axis_index("seq")
    one_back = shifted(attn_kv, "seq", 1)
    two_back = shifted(attn_kv, "seq", 2)
    window = jnp.concatenate([two_back, one_back, attn_kv], axis=0)
    first_row = block_index * count
    query_pos = first_row + jnp.arange(count, dtype=jnp.int32)
    key_pos = first_row - 2 * count + jnp.arange(3 * count, dtype=jnp.int32)
    attn_out = attend(attn_q, window, query_pos, key_pos)
    stream = (
        moe_in.astype(jnp.float32) + ssm_out.astype(jnp.float32) + attn_out.astype(jnp.float32)
    ).astype(jnp.bfloat16)
    local_tokens = stream.shape[0]
    width = stream.shape[1]
    seq_count = lax.axis_size("seq")
    group = seq_count // EXP_WIN
    expert_ids = jnp.arange(EXP_WIN, dtype=jnp.int32)
    matches = moe_routes[:, :, None] == expert_ids[None, None, :]
    routed = jnp.any(matches, axis=1).astype(jnp.int32)
    route_share = jnp.sum(jnp.where(matches, moe_prob[:, :, None], 0.0), axis=1)
    position_rank = jnp.cumsum(routed, axis=0) - 1
    picker = (routed[:, :, None] == 1) & (
        position_rank[:, :, None] == jnp.arange(CAP, dtype=jnp.int32)[None, None, :]
    )
    packed = jnp.einsum(
        "tek,td->ekd", picker.astype(jnp.bfloat16), stream, preferred_element_type=jnp.float32
    ).astype(jnp.bfloat16)
    outgoing = jnp.repeat(packed, group, axis=0)
    arrived = lax.all_to_all(outgoing, "seq", split_axis=0, concat_axis=0, tiled=True)
    gathered = arrived.reshape(-1, arrived.shape[-1])
    partial_value = expert_partial(gathered, w_gate, w_up, w_down)
    returned = lax.all_to_all(
        partial_value.reshape(arrived.shape), "seq", split_axis=0, concat_axis=0, tiled=True
    )
    summed = jnp.sum(returned.reshape(EXP_WIN, group, CAP, width), axis=1, dtype=jnp.float32)
    weighting = (picker.astype(jnp.float32) * route_share[:, :, None]).reshape(
        local_tokens, EXP_WIN * CAP
    )
    combined = jnp.dot(
        weighting,
        summed.reshape(EXP_WIN * CAP, width),
        precision=lax.Precision.HIGHEST,
        preferred_element_type=jnp.float32,
    )
    moe_out = combined.astype(jnp.bfloat16)
    return (ssm_out, attn_out, moe_out)


def solution(mesh):
    return jax.shard_map(
        body,
        mesh=mesh,
        in_specs=(
            P(("grp", "seq"), None),
            P(("grp", "seq"), None),
            P(),
            P(None, ("grp", "seq")),
            P(None, ("grp", "seq")),
            P(("grp", "seq"), None),
            P(("grp", "seq"), None),
            P(("grp", "seq"), None),
            P(("grp", "seq"), None),
            P(("grp", "seq"), None),
            P(None, "seq"),
            P(None, "seq"),
            P("seq", None),
        ),
        out_specs=(P(("grp", "seq"), None), P(("grp", "seq"), None), P(("grp", "seq"), None)),
        check_vma=False,
    )
```

```python
import math

import jax
import jax.numpy as jnp
from jax import lax
from jax.experimental import pallas as pl
from jax.experimental.pallas import tpu as pltpu
from jax.sharding import PartitionSpec as P

HQ = 32
HK = 8
HEAD_SIZE = 128
EXP_WIN = 4
CAP = 12


def shifted(value, axis, by, devices=None):
    devices = devices or lax.axis_size(axis)
    pairs = [(i, i + by) for i in range(devices) if 0 <= i + by < devices]
    return lax.ppermute(value, axis, pairs)


def scan_kernel(b_ref, c_ref, dt_ref, inj_ref, a_ref, read_ref, end_ref):
    states = a_ref.shape[0]
    steps = dt_ref.shape[0]
    h = [jnp.zeros(dt_ref.shape[1:], jnp.float32) for _ in range(states)]
    for t in range(steps):
        d = dt_ref[t]
        u = inj_ref[t]
        total = None
        for n in range(states):
            h[n] = jnp.exp(d * a_ref[n]) * h[n] + b_ref[n, t] * u
            term = c_ref[n, t] * h[n]
            total = term if total is None else total + term
        read_ref[t] = total
    for n in range(states):
        end_ref[n] = h[n]


def sweep(values, deltas, rates, inject_rows, read_rows):
    steps, channels = deltas.shape
    states = rates.shape[0]
    lanes = 128
    rows = channels // lanes
    tile = 8
    dt3 = deltas.reshape(steps, rows, lanes)
    inj3 = (deltas * values).reshape(steps, rows, lanes)
    a3 = rates.reshape(states, rows, lanes)
    read3, end3 = pl.pallas_call(
        scan_kernel,
        grid=(rows // tile,),
        in_specs=[
            pl.BlockSpec(memory_space=pltpu.SMEM),
            pl.BlockSpec(memory_space=pltpu.SMEM),
            pl.BlockSpec((steps, tile, lanes), lambda j: (0, j, 0)),
            pl.BlockSpec((steps, tile, lanes), lambda j: (0, j, 0)),
            pl.BlockSpec((states, tile, lanes), lambda j: (0, j, 0)),
        ],
        out_specs=[
            pl.BlockSpec((steps, tile, lanes), lambda j: (0, j, 0)),
            pl.BlockSpec((states, tile, lanes), lambda j: (0, j, 0)),
        ],
        out_shape=[
            jax.ShapeDtypeStruct((steps, rows, lanes), jnp.float32),
            jax.ShapeDtypeStruct((states, rows, lanes), jnp.float32),
        ],
    )(inject_rows, read_rows, dt3, inj3, a3)
    return end3.reshape(states, channels), read3.reshape(steps, channels)


def ssm_correct(local_read, local_end, deltas, rates, read_rows, devices):
    running = jnp.cumsum(deltas, axis=0)
    span = running[-1]

    def join(earlier, later):
        return (earlier[0] + later[0], jnp.exp(rates * later[0][None, :]) * earlier[1] + later[1])

    closest = (shifted(span, "seq", 1, devices), shifted(local_end, "seq", 1, devices))
    if devices > 2:
        before = (shifted(span, "seq", 2, devices), shifted(local_end, "seq", 2, devices))
        closest = join(before, closest)
    reach = 2
    while reach < devices:
        earlier = (shifted(closest[0], "seq", reach, devices), shifted(closest[1], "seq", reach, devices))
        closest = join(earlier, closest)
        reach *= 2
    incoming = closest[1]
    growth = jnp.exp(rates[None] * running[:, None, :]) * incoming[None]
    fix = jnp.sum(read_rows.T[:, :, None] * growth, axis=1)
    return (local_read + fix).astype(jnp.bfloat16)


def attend(queries, window, query_pos, key_pos):
    count = queries.shape[0]
    key_count = window.shape[0]
    repeat = HQ // HK
    query_head_tensor = queries.reshape(count, HK, repeat, HEAD_SIZE)
    key_head_tensor = window[:, : HK * HEAD_SIZE].reshape(key_count, HK, HEAD_SIZE)
    value_head_tensor = window[:, HK * HEAD_SIZE :].reshape(key_count, HK, HEAD_SIZE)
    attention_scores = jnp.einsum(
        "bajq,oaq->ajbo", query_head_tensor, key_head_tensor, preferred_element_type=jnp.float32
    ) / math.sqrt(HEAD_SIZE)
    allowed = (key_pos[None, :] >= 0) & (key_pos[None, :] <= query_pos[:, None])
    attention_scores = jnp.where(allowed[None, None], attention_scores, -jnp.inf)
    row_max = jnp.max(attention_scores, axis=-1, keepdims=True)
    expd = jnp.exp(attention_scores - row_max)
    probabilities = (expd / jnp.sum(expd, axis=-1, keepdims=True)).astype(jnp.bfloat16)
    expert_mixture = jnp.einsum(
        "kyje,eku->jkyu", probabilities, value_head_tensor, preferred_element_type=jnp.float32
    )
    return expert_mixture.reshape(count, HQ * HEAD_SIZE).astype(jnp.bfloat16)


def expert_partial(gathered, w_gate, w_up, w_down):
    gate_pre = jnp.dot(gathered, w_gate, preferred_element_type=jnp.float32)
    up_pre = jnp.dot(gathered, w_up, preferred_element_type=jnp.float32)
    hidden_act = (jax.nn.silu(gate_pre) * up_pre).astype(jnp.bfloat16)
    return jnp.dot(hidden_act, w_down, preferred_element_type=jnp.float32).astype(jnp.bfloat16)


def body(
    ssm_in,
    ssm_dt,
    ssm_a,
    ssm_b,
    ssm_c,
    attn_q,
    attn_kv,
    moe_in,
    moe_routes,
    moe_prob,
    w_gate,
    w_up,
    w_down,
):
    values = ssm_in.astype(jnp.float32)
    deltas = ssm_dt.astype(jnp.float32)
    local_end, local_read = sweep(values, deltas, ssm_a, ssm_b, ssm_c)
    ssm_out = ssm_correct(local_read, local_end, deltas, ssm_a, ssm_c, lax.axis_size("seq"))
    count = attn_q.shape[0]
    block_index = lax.axis_index("seq")
    one_back = shifted(attn_kv, "seq", 1)
    two_back = shifted(attn_kv, "seq", 2)
    window = jnp.concatenate([two_back, one_back, attn_kv], axis=0)
    first_row = block_index * count
    query_pos = first_row + jnp.arange(count, dtype=jnp.int32)
    key_pos = first_row - 2 * count + jnp.arange(3 * count, dtype=jnp.int32)
    attn_out = attend(attn_q, window, query_pos, key_pos)
    stream = (
        moe_in.astype(jnp.float32) + ssm_out.astype(jnp.float32) + attn_out.astype(jnp.float32)
    ).astype(jnp.bfloat16)
    local_tokens = stream.shape[0]
    width = stream.shape[1]
    seq_count = lax.axis_size("seq")
    group = seq_count // EXP_WIN
    expert_ids = jnp.arange(EXP_WIN, dtype=jnp.int32)
    matches = moe_routes[:, :, None] == expert_ids[None, None, :]
    routed = jnp.any(matches, axis=1).astype(jnp.int32)
    route_share = jnp.sum(jnp.where(matches, moe_prob[:, :, None], 0.0), axis=1)
    position_rank = jnp.cumsum(routed, axis=0) - 1
    picker = (routed[:, :, None] == 1) & (
        position_rank[:, :, None] == jnp.arange(CAP, dtype=jnp.int32)[None, None, :]
    )
    packed = jnp.einsum(
        "tek,td->ekd", picker.astype(jnp.bfloat16), stream, preferred_element_type=jnp.float32
    ).astype(jnp.bfloat16)
    outgoing = jnp.repeat(packed, group, axis=0)
    arrived = lax.all_to_all(outgoing, "seq", split_axis=0, concat_axis=0, tiled=True)
    gathered = arrived.reshape(-1, arrived.shape[-1])
    partial_value = expert_partial(gathered, w_gate, w_up, w_down)
    returned = lax.all_to_all(
        partial_value.reshape(arrived.shape), "seq", split_axis=0, concat_axis=0, tiled=True
    )
    summed = jnp.sum(returned.reshape(EXP_WIN, group, CAP, width), axis=1, dtype=jnp.float32)
    weighting = (picker.astype(jnp.float32) * route_share[:, :, None]).reshape(
        local_tokens, EXP_WIN * CAP
    )
    combined = jnp.dot(
        weighting,
        summed.reshape(EXP_WIN * CAP, width),
        precision=lax.Precision.HIGHEST,
        preferred_element_type=jnp.float32,
    )
    moe_out = combined.astype(jnp.bfloat16)
    return (ssm_out, attn_out, moe_out)


def solution(mesh):
    return jax.shard_map(
        body,
        mesh=mesh,
        in_specs=(
            P(("grp", "seq"), None),
            P(("grp", "seq"), None),
            P(),
            P(None, ("grp", "seq")),
            P(None, ("grp", "seq")),
            P(("grp", "seq"), None),
            P(("grp", "seq"), None),
            P(("grp", "seq"), None),
            P(("grp", "seq"), None),
            P(("grp", "seq"), None),
            P(None, "seq"),
            P(None, "seq"),
            P("seq", None),
        ),
        out_specs=(P(("grp", "seq"), None), P(("grp", "seq"), None), P(("grp", "seq"), None)),
        check_vma=False,
    )
```

```python
import math

import jax
import jax.numpy as jnp
from jax import lax
from jax.experimental import pallas as pl
from jax.experimental.pallas import tpu as pltpu
from jax.sharding import PartitionSpec as P

HQ = 32
HK = 8
HEAD_SIZE = 128
EXP_WIN = 4
CAP = 12
SLOTS = -(-CAP // 16) * 16


def shifted(value, axis, by):
    devices = lax.axis_size(axis)
    pairs = [(i, i + by) for i in range(devices) if 0 <= i + by < devices]
    return lax.ppermute(value, axis, pairs)


def scan_kernel(b_ref, c_ref, dt_ref, inj_ref, a_ref, read_ref, end_ref):
    states = a_ref.shape[0]
    steps = dt_ref.shape[0]
    h = [jnp.zeros(dt_ref.shape[1:], jnp.float32) for _ in range(states)]
    for t in range(steps):
        d = dt_ref[t]
        u = inj_ref[t]
        total = None
        for n in range(states):
            h[n] = jnp.exp(d * a_ref[n]) * h[n] + b_ref[n, t] * u
            term = c_ref[n, t] * h[n]
            total = term if total is None else total + term
        read_ref[t] = total
    for n in range(states):
        end_ref[n] = h[n]


def sweep(values, deltas, rates, inject_rows, read_rows):
    steps, channels = deltas.shape
    states = rates.shape[0]
    lanes = 128
    rows = channels // lanes
    tile = 8
    dt3 = deltas.reshape(steps, rows, lanes)
    inj3 = (deltas * values).reshape(steps, rows, lanes)
    a3 = rates.reshape(states, rows, lanes)
    read3, end3 = pl.pallas_call(
        scan_kernel,
        grid=(rows // tile,),
        in_specs=[
            pl.BlockSpec(memory_space=pltpu.SMEM),
            pl.BlockSpec(memory_space=pltpu.SMEM),
            pl.BlockSpec((steps, tile, lanes), lambda j: (0, j, 0)),
            pl.BlockSpec((steps, tile, lanes), lambda j: (0, j, 0)),
            pl.BlockSpec((states, tile, lanes), lambda j: (0, j, 0)),
        ],
        out_specs=[
            pl.BlockSpec((steps, tile, lanes), lambda j: (0, j, 0)),
            pl.BlockSpec((states, tile, lanes), lambda j: (0, j, 0)),
        ],
        out_shape=[
            jax.ShapeDtypeStruct((steps, rows, lanes), jnp.float32),
            jax.ShapeDtypeStruct((states, rows, lanes), jnp.float32),
        ],
    )(inject_rows, read_rows, dt3, inj3, a3)
    return end3.reshape(states, channels), read3.reshape(steps, channels)


def ssm_correct(local_read, local_end, deltas, rates, read_rows):
    mine = lax.axis_index("seq")
    running = jnp.cumsum(deltas, axis=0)
    ends = lax.all_gather(local_end, "seq")
    sums = lax.all_gather(running[-1], "seq")
    devices = sums.shape[0]
    order = jnp.arange(devices, dtype=jnp.int32)
    masked = jnp.where((order < mine)[:, None], sums, 0.0)
    after = jnp.sum(masked, axis=0)[None, :] - jnp.cumsum(masked, axis=0)
    after = jnp.maximum(after, 0.0)
    carry = jnp.exp(rates[None] * after[:, None, :]) * ends
    incoming = jnp.sum(jnp.where((order < mine)[:, None, None], carry, 0.0), axis=0)
    growth = jnp.exp(rates[None] * running[:, None, :]) * incoming[None]
    fix = jnp.sum(read_rows.T[:, :, None] * growth, axis=1)
    return (local_read + fix).astype(jnp.bfloat16)


def attend(queries, window, query_pos, key_pos):
    count = queries.shape[0]
    key_count = window.shape[0]
    repeat = HQ // HK
    query_head_tensor = queries.reshape(count, HK, repeat, HEAD_SIZE)
    key_head_tensor = window[:, : HK * HEAD_SIZE].reshape(key_count, HK, HEAD_SIZE)
    value_head_tensor = window[:, HK * HEAD_SIZE :].reshape(key_count, HK, HEAD_SIZE)
    attention_scores = jnp.einsum(
        "bajq,oaq->ajbo", query_head_tensor, key_head_tensor, preferred_element_type=jnp.float32
    ) / math.sqrt(HEAD_SIZE)
    allowed = (key_pos[None, :] >= 0) & (key_pos[None, :] <= query_pos[:, None])
    attention_scores = jnp.where(allowed[None, None], attention_scores, -jnp.inf)
    row_max = jnp.max(attention_scores, axis=-1, keepdims=True)
    expd = jnp.exp(attention_scores - row_max)
    probabilities = (expd / jnp.sum(expd, axis=-1, keepdims=True)).astype(jnp.bfloat16)
    expert_mixture = jnp.einsum(
        "kyje,eku->jkyu", probabilities, value_head_tensor, preferred_element_type=jnp.float32
    )
    return expert_mixture.reshape(count, HQ * HEAD_SIZE).astype(jnp.bfloat16)


def expert_partial(gathered, w_gate, w_up, w_down):
    gate_pre = jnp.dot(gathered, w_gate, preferred_element_type=jnp.float32)
    up_pre = jnp.dot(gathered, w_up, preferred_element_type=jnp.float32)
    hidden_act = (jax.nn.silu(gate_pre) * up_pre).astype(jnp.bfloat16)
    return jnp.dot(hidden_act, w_down, preferred_element_type=jnp.float32).astype(jnp.bfloat16)


def body(
    ssm_in,
    ssm_dt,
    ssm_a,
    ssm_b,
    ssm_c,
    attn_q,
    attn_kv,
    moe_in,
    moe_routes,
    moe_prob,
    w_gate,
    w_up,
    w_down,
):
    values = ssm_in.astype(jnp.float32)
    deltas = ssm_dt.astype(jnp.float32)
    local_end, local_read = sweep(values, deltas, ssm_a, ssm_b, ssm_c)
    ssm_out = ssm_correct(local_read, local_end, deltas, ssm_a, ssm_c)
    count = attn_q.shape[0]
    block_index = lax.axis_index("seq")
    one_back = shifted(attn_kv, "seq", 1)
    two_back = shifted(attn_kv, "seq", 2)
    window = jnp.concatenate([two_back, one_back, attn_kv], axis=0)
    first_row = block_index * count
    query_pos = first_row + jnp.arange(count, dtype=jnp.int32)
    key_pos = first_row - 2 * count + jnp.arange(3 * count, dtype=jnp.int32)
    attn_out = attend(attn_q, window, query_pos, key_pos)
    stream = (
        moe_in.astype(jnp.float32) + ssm_out.astype(jnp.float32) + attn_out.astype(jnp.float32)
    ).astype(jnp.bfloat16)
    local_tokens = stream.shape[0]
    width = stream.shape[1]
    seq_count = lax.axis_size("seq")
    group = seq_count // EXP_WIN
    expert_ids = jnp.arange(EXP_WIN, dtype=jnp.int32)
    matches = moe_routes[:, :, None] == expert_ids[None, None, :]
    routed = jnp.any(matches, axis=1).astype(jnp.int32)
    route_share = jnp.sum(jnp.where(matches, moe_prob[:, :, None], 0.0), axis=1)
    position_rank = jnp.cumsum(routed, axis=0) - 1
    picker = (routed[:, :, None] == 1) & (
        position_rank[:, :, None] == jnp.arange(SLOTS, dtype=jnp.int32)[None, None, :]
    )
    packed = jnp.einsum(
        "tek,td->ekd", picker.astype(jnp.bfloat16), stream, preferred_element_type=jnp.float32
    ).astype(jnp.bfloat16)
    outgoing = jnp.repeat(packed, group, axis=0)
    arrived = lax.all_to_all(outgoing, "seq", split_axis=0, concat_axis=0, tiled=True)
    gathered = arrived.reshape(-1, arrived.shape[-1])
    partial_value = expert_partial(gathered, w_gate, w_up, w_down)
    returned = lax.all_to_all(
        partial_value.reshape(arrived.shape), "seq", split_axis=0, concat_axis=0, tiled=True
    )
    summed = jnp.sum(returned.reshape(EXP_WIN, group, SLOTS, width), axis=1, dtype=jnp.float32)
    weighting = (picker.astype(jnp.float32) * route_share[:, :, None]).reshape(
        local_tokens, EXP_WIN * SLOTS
    )
    combined = jnp.dot(
        weighting,
        summed.reshape(EXP_WIN * SLOTS, width),
        precision=lax.Precision.HIGHEST,
        preferred_element_type=jnp.float32,
    )
    moe_out = combined.astype(jnp.bfloat16)
    return (ssm_out, attn_out, moe_out)


def solution(mesh):
    return jax.shard_map(
        body,
        mesh=mesh,
        in_specs=(
            P(("grp", "seq"), None),
            P(("grp", "seq"), None),
            P(),
            P(None, ("grp", "seq")),
            P(None, ("grp", "seq")),
            P(("grp", "seq"), None),
            P(("grp", "seq"), None),
            P(("grp", "seq"), None),
            P(("grp", "seq"), None),
            P(("grp", "seq"), None),
            P(None, "seq"),
            P(None, "seq"),
            P("seq", None),
        ),
        out_specs=(P(("grp", "seq"), None), P(("grp", "seq"), None), P(("grp", "seq"), None)),
        check_vma=False,
    )
```

```python
import math

import jax
import jax.numpy as jnp
from jax import lax
from jax.experimental import pallas as pl
from jax.experimental.pallas import tpu as pltpu
from jax.sharding import PartitionSpec as P

HQ = 32
HK = 8
HEAD_SIZE = 128
EXP_WIN = 4
CAP = 12
SLOTS = -(-CAP // 16) * 16


def shifted(value, axis, by):
    devices = lax.axis_size(axis)
    pairs = [(i, i + by) for i in range(devices) if 0 <= i + by < devices]
    return lax.ppermute(value, axis, pairs)


def scan_kernel(b_ref, c_ref, dt_ref, inj_ref, a_ref, read_ref, end_ref):
    states = a_ref.shape[0]
    steps = dt_ref.shape[0]
    h = [jnp.zeros(dt_ref.shape[1:], jnp.float32) for _ in range(states)]
    for t in range(steps):
        d = dt_ref[t]
        u = inj_ref[t]
        total = None
        for n in range(states):
            h[n] = jnp.exp(d * a_ref[n]) * h[n] + b_ref[n, t] * u
            term = c_ref[n, t] * h[n]
            total = term if total is None else total + term
        read_ref[t] = total
    for n in range(states):
        end_ref[n] = h[n]


def sweep(values, deltas, rates, inject_rows, read_rows):
    steps, channels = deltas.shape
    states = rates.shape[0]
    lanes = 128
    rows = channels // lanes
    tile = 8
    dt3 = deltas.reshape(steps, rows, lanes)
    inj3 = (deltas * values).reshape(steps, rows, lanes)
    a3 = rates.reshape(states, rows, lanes)
    read3, end3 = pl.pallas_call(
        scan_kernel,
        grid=(rows // tile,),
        in_specs=[
            pl.BlockSpec(memory_space=pltpu.SMEM),
            pl.BlockSpec(memory_space=pltpu.SMEM),
            pl.BlockSpec((steps, tile, lanes), lambda j: (0, j, 0)),
            pl.BlockSpec((steps, tile, lanes), lambda j: (0, j, 0)),
            pl.BlockSpec((states, tile, lanes), lambda j: (0, j, 0)),
        ],
        out_specs=[
            pl.BlockSpec((steps, tile, lanes), lambda j: (0, j, 0)),
            pl.BlockSpec((states, tile, lanes), lambda j: (0, j, 0)),
        ],
        out_shape=[
            jax.ShapeDtypeStruct((steps, rows, lanes), jnp.float32),
            jax.ShapeDtypeStruct((states, rows, lanes), jnp.float32),
        ],
    )(inject_rows, read_rows, dt3, inj3, a3)
    return end3.reshape(states, channels), read3.reshape(steps, channels)


def ssm_correct(local_read, local_end, deltas, rates, read_rows):
    mine = lax.axis_index("seq")
    running = jnp.cumsum(deltas, axis=0)
    ends = lax.all_gather(local_end.astype(jnp.bfloat16), "seq").astype(jnp.float32)
    sums = lax.all_gather(running[-1], "seq")
    devices = sums.shape[0]
    order = jnp.arange(devices, dtype=jnp.int32)
    masked = jnp.where((order < mine)[:, None], sums, 0.0)
    after = jnp.sum(masked, axis=0)[None, :] - jnp.cumsum(masked, axis=0)
    after = jnp.maximum(after, 0.0)
    carry = jnp.exp(rates[None] * after[:, None, :]) * ends
    incoming = jnp.sum(jnp.where((order < mine)[:, None, None], carry, 0.0), axis=0)
    growth = jnp.exp(rates[None] * running[:, None, :]) * incoming[None]
    fix = jnp.sum(read_rows.T[:, :, None] * growth, axis=1)
    return (local_read + fix).astype(jnp.bfloat16)


def attend(queries, window, query_pos, key_pos):
    count = queries.shape[0]
    key_count = window.shape[0]
    repeat = HQ // HK
    query_head_tensor = queries.reshape(count, HK, repeat, HEAD_SIZE)
    key_head_tensor = window[:, : HK * HEAD_SIZE].reshape(key_count, HK, HEAD_SIZE)
    value_head_tensor = window[:, HK * HEAD_SIZE :].reshape(key_count, HK, HEAD_SIZE)
    attention_scores = jnp.einsum(
        "bajq,oaq->ajbo", query_head_tensor, key_head_tensor, preferred_element_type=jnp.float32
    ) / math.sqrt(HEAD_SIZE)
    allowed = (key_pos[None, :] >= 0) & (key_pos[None, :] <= query_pos[:, None])
    attention_scores = jnp.where(allowed[None, None], attention_scores, -jnp.inf)
    row_max = jnp.max(attention_scores, axis=-1, keepdims=True)
    expd = jnp.exp(attention_scores - row_max)
    probabilities = (expd / jnp.sum(expd, axis=-1, keepdims=True)).astype(jnp.bfloat16)
    expert_mixture = jnp.einsum(
        "kyje,eku->jkyu", probabilities, value_head_tensor, preferred_element_type=jnp.float32
    )
    return expert_mixture.reshape(count, HQ * HEAD_SIZE).astype(jnp.bfloat16)


def expert_partial(gathered, w_gate, w_up, w_down):
    gate_pre = jnp.dot(gathered, w_gate, preferred_element_type=jnp.float32)
    up_pre = jnp.dot(gathered, w_up, preferred_element_type=jnp.float32)
    hidden_act = (jax.nn.silu(gate_pre) * up_pre).astype(jnp.bfloat16)
    return jnp.dot(hidden_act, w_down, preferred_element_type=jnp.float32).astype(jnp.bfloat16)


def body(
    ssm_in,
    ssm_dt,
    ssm_a,
    ssm_b,
    ssm_c,
    attn_q,
    attn_kv,
    moe_in,
    moe_routes,
    moe_prob,
    w_gate,
    w_up,
    w_down,
):
    values = ssm_in.astype(jnp.float32)
    deltas = ssm_dt.astype(jnp.float32)
    local_end, local_read = sweep(values, deltas, ssm_a, ssm_b, ssm_c)
    ssm_out = ssm_correct(local_read, local_end, deltas, ssm_a, ssm_c)
    count = attn_q.shape[0]
    block_index = lax.axis_index("seq")
    one_back = shifted(attn_kv, "seq", 1)
    two_back = shifted(attn_kv, "seq", 2)
    window = jnp.concatenate([two_back, one_back, attn_kv], axis=0)
    first_row = block_index * count
    query_pos = first_row + jnp.arange(count, dtype=jnp.int32)
    key_pos = first_row - 2 * count + jnp.arange(3 * count, dtype=jnp.int32)
    attn_out = attend(attn_q, window, query_pos, key_pos)
    stream = (
        moe_in.astype(jnp.float32) + ssm_out.astype(jnp.float32) + attn_out.astype(jnp.float32)
    ).astype(jnp.bfloat16)
    local_tokens = stream.shape[0]
    width = stream.shape[1]
    seq_count = lax.axis_size("seq")
    group = seq_count // EXP_WIN
    expert_ids = jnp.arange(EXP_WIN, dtype=jnp.int32)
    matches = moe_routes[:, :, None] == expert_ids[None, None, :]
    routed = jnp.any(matches, axis=1).astype(jnp.int32)
    route_share = jnp.sum(jnp.where(matches, moe_prob[:, :, None], 0.0), axis=1)
    position_rank = jnp.cumsum(routed, axis=0) - 1
    picker = (routed[:, :, None] == 1) & (
        position_rank[:, :, None] == jnp.arange(SLOTS, dtype=jnp.int32)[None, None, :]
    )
    packed = jnp.einsum(
        "tek,td->ekd", picker.astype(jnp.bfloat16), stream, preferred_element_type=jnp.float32
    ).astype(jnp.bfloat16)
    outgoing = jnp.repeat(packed, group, axis=0)
    arrived = lax.all_to_all(outgoing, "seq", split_axis=0, concat_axis=0, tiled=True)
    gathered = arrived.reshape(-1, arrived.shape[-1])
    partial_value = expert_partial(gathered, w_gate, w_up, w_down)
    returned = lax.all_to_all(
        partial_value.reshape(arrived.shape), "seq", split_axis=0, concat_axis=0, tiled=True
    )
    summed = jnp.sum(returned.reshape(EXP_WIN, group, SLOTS, width), axis=1, dtype=jnp.float32)
    weighting = (picker.astype(jnp.float32) * route_share[:, :, None]).reshape(
        local_tokens, EXP_WIN * SLOTS
    )
    combined = jnp.dot(
        weighting,
        summed.reshape(EXP_WIN * SLOTS, width),
        precision=lax.Precision.HIGHEST,
        preferred_element_type=jnp.float32,
    )
    moe_out = combined.astype(jnp.bfloat16)
    return (ssm_out, attn_out, moe_out)


def solution(mesh):
    return jax.shard_map(
        body,
        mesh=mesh,
        in_specs=(
            P(("grp", "seq"), None),
            P(("grp", "seq"), None),
            P(),
            P(None, ("grp", "seq")),
            P(None, ("grp", "seq")),
            P(("grp", "seq"), None),
            P(("grp", "seq"), None),
            P(("grp", "seq"), None),
            P(("grp", "seq"), None),
            P(("grp", "seq"), None),
            P(None, "seq"),
            P(None, "seq"),
            P("seq", None),
        ),
        out_specs=(P(("grp", "seq"), None), P(("grp", "seq"), None), P(("grp", "seq"), None)),
        check_vma=False,
    )
```

```python
import functools
import math

import jax
import jax.numpy as jnp
from jax import lax
from jax.experimental import pallas as pl
from jax.experimental.pallas import tpu as pltpu
from jax.sharding import Mesh, PartitionSpec as P

HQ = 32
HK = 8
HEAD_SIZE = 128
EXP_WIN = 4
CAP = 12
SLOTS = -(-CAP // 16) * 16
SEQ = ("eg", "kg")


def shifted(value, axis, by, devices):
    pairs = [(i, i + by) for i in range(devices) if 0 <= i + by < devices]
    return lax.ppermute(value, axis, pairs)


def scan_kernel(b_ref, c_ref, dt_ref, inj_ref, a_ref, read_ref, end_ref):
    states = a_ref.shape[0]
    steps = dt_ref.shape[0]
    h = [jnp.zeros(dt_ref.shape[1:], jnp.float32) for _ in range(states)]
    for t in range(steps):
        d = dt_ref[t]
        u = inj_ref[t]
        total = None
        for n in range(states):
            h[n] = jnp.exp(d * a_ref[n]) * h[n] + b_ref[n, t] * u
            term = c_ref[n, t] * h[n]
            total = term if total is None else total + term
        read_ref[t] = total
    for n in range(states):
        end_ref[n] = h[n]


def sweep(values, deltas, rates, inject_rows, read_rows):
    steps, channels = deltas.shape
    states = rates.shape[0]
    lanes = 128
    rows = channels // lanes
    tile = 8
    dt3 = deltas.reshape(steps, rows, lanes)
    inj3 = (deltas * values).reshape(steps, rows, lanes)
    a3 = rates.reshape(states, rows, lanes)
    read3, end3 = pl.pallas_call(
        scan_kernel,
        grid=(rows // tile,),
        in_specs=[
            pl.BlockSpec(memory_space=pltpu.SMEM),
            pl.BlockSpec(memory_space=pltpu.SMEM),
            pl.BlockSpec((steps, tile, lanes), lambda j: (0, j, 0)),
            pl.BlockSpec((steps, tile, lanes), lambda j: (0, j, 0)),
            pl.BlockSpec((states, tile, lanes), lambda j: (0, j, 0)),
        ],
        out_specs=[
            pl.BlockSpec((steps, tile, lanes), lambda j: (0, j, 0)),
            pl.BlockSpec((states, tile, lanes), lambda j: (0, j, 0)),
        ],
        out_shape=[
            jax.ShapeDtypeStruct((steps, rows, lanes), jnp.float32),
            jax.ShapeDtypeStruct((states, rows, lanes), jnp.float32),
        ],
    )(inject_rows, read_rows, dt3, inj3, a3)
    return end3.reshape(states, channels), read3.reshape(steps, channels)


def ssm_correct(local_read, local_end, deltas, rates, read_rows):
    mine = lax.axis_index(SEQ)
    running = jnp.cumsum(deltas, axis=0)
    ends = lax.all_gather(local_end, SEQ)
    sums = lax.all_gather(running[-1], SEQ)
    devices = sums.shape[0]
    order = jnp.arange(devices, dtype=jnp.int32)
    masked = jnp.where((order < mine)[:, None], sums, 0.0)
    after = jnp.sum(masked, axis=0)[None, :] - jnp.cumsum(masked, axis=0)
    after = jnp.maximum(after, 0.0)
    carry = jnp.exp(rates[None] * after[:, None, :]) * ends
    incoming = jnp.sum(jnp.where((order < mine)[:, None, None], carry, 0.0), axis=0)
    growth = jnp.exp(rates[None] * running[:, None, :]) * incoming[None]
    fix = jnp.sum(read_rows.T[:, :, None] * growth, axis=1)
    return (local_read + fix).astype(jnp.bfloat16)


def attend(queries, window, query_pos, key_pos):
    count = queries.shape[0]
    key_count = window.shape[0]
    repeat = HQ // HK
    query_head_tensor = queries.reshape(count, HK, repeat, HEAD_SIZE)
    key_head_tensor = window[:, : HK * HEAD_SIZE].reshape(key_count, HK, HEAD_SIZE)
    value_head_tensor = window[:, HK * HEAD_SIZE :].reshape(key_count, HK, HEAD_SIZE)
    attention_scores = jnp.einsum(
        "bajq,oaq->ajbo", query_head_tensor, key_head_tensor, preferred_element_type=jnp.float32
    ) / math.sqrt(HEAD_SIZE)
    allowed = (key_pos[None, :] >= 0) & (key_pos[None, :] <= query_pos[:, None])
    attention_scores = jnp.where(allowed[None, None], attention_scores, -jnp.inf)
    row_max = jnp.max(attention_scores, axis=-1, keepdims=True)
    expd = jnp.exp(attention_scores - row_max)
    probabilities = (expd / jnp.sum(expd, axis=-1, keepdims=True)).astype(jnp.bfloat16)
    expert_mixture = jnp.einsum(
        "kyje,eku->jkyu", probabilities, value_head_tensor, preferred_element_type=jnp.float32
    )
    return expert_mixture.reshape(count, HQ * HEAD_SIZE).astype(jnp.bfloat16)


def expert_partial(gathered, w_gate, w_up, w_down):
    gate_pre = jnp.dot(gathered, w_gate, preferred_element_type=jnp.float32)
    up_pre = jnp.dot(gathered, w_up, preferred_element_type=jnp.float32)
    hidden_act = (jax.nn.silu(gate_pre) * up_pre).astype(jnp.bfloat16)
    return jnp.dot(hidden_act, w_down, preferred_element_type=jnp.float32).astype(jnp.bfloat16)


def body(
    ssm_in,
    ssm_dt,
    ssm_a,
    ssm_b,
    ssm_c,
    attn_q,
    attn_kv,
    moe_in,
    moe_routes,
    moe_prob,
    w_gate,
    w_up,
    w_down,
    *,
    seq_count,
):
    values = ssm_in.astype(jnp.float32)
    deltas = ssm_dt.astype(jnp.float32)
    local_end, local_read = sweep(values, deltas, ssm_a, ssm_b, ssm_c)
    ssm_out = ssm_correct(local_read, local_end, deltas, ssm_a, ssm_c)
    count = attn_q.shape[0]
    block_index = lax.axis_index(SEQ)
    one_back = shifted(attn_kv, SEQ, 1, seq_count)
    two_back = shifted(attn_kv, SEQ, 2, seq_count)
    window = jnp.concatenate([two_back, one_back, attn_kv], axis=0)
    first_row = block_index * count
    query_pos = first_row + jnp.arange(count, dtype=jnp.int32)
    key_pos = first_row - 2 * count + jnp.arange(3 * count, dtype=jnp.int32)
    attn_out = attend(attn_q, window, query_pos, key_pos)
    stream = (
        moe_in.astype(jnp.float32) + ssm_out.astype(jnp.float32) + attn_out.astype(jnp.float32)
    ).astype(jnp.bfloat16)
    local_tokens = stream.shape[0]
    width = stream.shape[1]
    group = seq_count // EXP_WIN
    expert_ids = jnp.arange(EXP_WIN, dtype=jnp.int32)
    matches = moe_routes[:, :, None] == expert_ids[None, None, :]
    routed = jnp.any(matches, axis=1).astype(jnp.int32)
    route_share = jnp.sum(jnp.where(matches, moe_prob[:, :, None], 0.0), axis=1)
    position_rank = jnp.cumsum(routed, axis=0) - 1
    picker = (routed[:, :, None] == 1) & (
        position_rank[:, :, None] == jnp.arange(SLOTS, dtype=jnp.int32)[None, None, :]
    )
    packed = jnp.einsum(
        "tek,td->ekd", picker.astype(jnp.bfloat16), stream, preferred_element_type=jnp.float32
    ).astype(jnp.bfloat16)
    by_expert = lax.all_to_all(packed, "eg", split_axis=0, concat_axis=0, tiled=True)
    outgoing = jnp.broadcast_to(by_expert[None], (group,) + by_expert.shape)
    arrived = lax.all_to_all(outgoing, "kg", split_axis=0, concat_axis=0, tiled=True)
    gathered = arrived.reshape(-1, width)
    partial_value = expert_partial(gathered, w_gate, w_up, w_down)
    blocks = lax.all_to_all(
        partial_value.reshape(arrived.shape), "kg", split_axis=0, concat_axis=0, tiled=True
    )
    block_sum = jnp.sum(blocks, axis=0, dtype=jnp.float32)
    summed = lax.all_to_all(block_sum, "eg", split_axis=0, concat_axis=0, tiled=True)
    weighting = (picker.astype(jnp.float32) * route_share[:, :, None]).reshape(
        local_tokens, EXP_WIN * SLOTS
    )
    combined = jnp.dot(
        weighting,
        summed.reshape(EXP_WIN * SLOTS, width),
        precision=lax.Precision.HIGHEST,
        preferred_element_type=jnp.float32,
    )
    moe_out = combined.astype(jnp.bfloat16)
    return (ssm_out, attn_out, moe_out)


def solution(mesh):
    groups = mesh.shape["grp"]
    seq_count = mesh.shape["seq"]
    fine = Mesh(
        mesh.devices.reshape(groups, EXP_WIN, seq_count // EXP_WIN), ("grp",) + SEQ
    )
    rows = P(("grp",) + SEQ, None)
    return jax.shard_map(
        functools.partial(body, seq_count=seq_count),
        mesh=fine,
        in_specs=(
            rows,
            rows,
            P(),
            P(None, ("grp",) + SEQ),
            P(None, ("grp",) + SEQ),
            rows,
            rows,
            rows,
            rows,
            rows,
            P(None, SEQ),
            P(None, SEQ),
            P(SEQ, None),
        ),
        out_specs=(rows, rows, rows),
        check_vma=False,
    )
```

```python
import functools
import math

import jax
import jax.numpy as jnp
from jax import lax
from jax.experimental import pallas as pl
from jax.experimental.pallas import tpu as pltpu
from jax.sharding import Mesh, PartitionSpec as P

HQ = 32
HK = 8
HEAD_SIZE = 128
EXP_WIN = 4
CAP = 12
SLOTS = -(-CAP // 16) * 16
SEQ = ("eg", "kg")


def shifted(value, axis, by, devices):
    pairs = [(i, i + by) for i in range(devices) if 0 <= i + by < devices]
    return lax.ppermute(value, axis, pairs)


def scan_kernel(b_ref, c_ref, dt_ref, inj_ref, a_ref, read_ref, end_ref):
    states = a_ref.shape[0]
    steps = dt_ref.shape[0]
    h = [jnp.zeros(dt_ref.shape[1:], jnp.float32) for _ in range(states)]
    for t in range(steps):
        d = dt_ref[t]
        u = inj_ref[t]
        total = None
        for n in range(states):
            h[n] = jnp.exp(d * a_ref[n]) * h[n] + b_ref[n, t] * u
            term = c_ref[n, t] * h[n]
            total = term if total is None else total + term
        read_ref[t] = total
    for n in range(states):
        end_ref[n] = h[n]


def sweep(values, deltas, rates, inject_rows, read_rows):
    steps, channels = deltas.shape
    states = rates.shape[0]
    lanes = 128
    rows = channels // lanes
    tile = 8
    dt3 = deltas.reshape(steps, rows, lanes)
    inj3 = (deltas * values).reshape(steps, rows, lanes)
    a3 = rates.reshape(states, rows, lanes)
    read3, end3 = pl.pallas_call(
        scan_kernel,
        grid=(rows // tile,),
        in_specs=[
            pl.BlockSpec(memory_space=pltpu.SMEM),
            pl.BlockSpec(memory_space=pltpu.SMEM),
            pl.BlockSpec((steps, tile, lanes), lambda j: (0, j, 0)),
            pl.BlockSpec((steps, tile, lanes), lambda j: (0, j, 0)),
            pl.BlockSpec((states, tile, lanes), lambda j: (0, j, 0)),
        ],
        out_specs=[
            pl.BlockSpec((steps, tile, lanes), lambda j: (0, j, 0)),
            pl.BlockSpec((states, tile, lanes), lambda j: (0, j, 0)),
        ],
        out_shape=[
            jax.ShapeDtypeStruct((steps, rows, lanes), jnp.float32),
            jax.ShapeDtypeStruct((states, rows, lanes), jnp.float32),
        ],
    )(inject_rows, read_rows, dt3, inj3, a3)
    return end3.reshape(states, channels), read3.reshape(steps, channels)


def ssm_correct(local_read, local_end, deltas, rates, read_rows):
    mine = lax.axis_index(SEQ)
    running = jnp.cumsum(deltas, axis=0)
    ends = lax.all_gather(local_end, SEQ)
    sums = lax.all_gather(running[-1], SEQ)
    devices = sums.shape[0]
    order = jnp.arange(devices, dtype=jnp.int32)
    masked = jnp.where((order < mine)[:, None], sums, 0.0)
    after = jnp.sum(masked, axis=0)[None, :] - jnp.cumsum(masked, axis=0)
    after = jnp.maximum(after, 0.0)
    carry = jnp.exp(rates[None] * after[:, None, :]) * ends
    incoming = jnp.sum(jnp.where((order < mine)[:, None, None], carry, 0.0), axis=0)
    growth = jnp.exp(rates[None] * running[:, None, :]) * incoming[None]
    fix = jnp.sum(read_rows.T[:, :, None] * growth, axis=1)
    return (local_read + fix).astype(jnp.bfloat16)


def attend(queries, window, query_pos, key_pos):
    count = queries.shape[0]
    key_count = window.shape[0]
    repeat = HQ // HK
    query_head_tensor = queries.reshape(count, HK, repeat, HEAD_SIZE)
    key_head_tensor = window[:, : HK * HEAD_SIZE].reshape(key_count, HK, HEAD_SIZE)
    value_head_tensor = window[:, HK * HEAD_SIZE :].reshape(key_count, HK, HEAD_SIZE)
    attention_scores = jnp.einsum(
        "bajq,oaq->ajbo", query_head_tensor, key_head_tensor, preferred_element_type=jnp.float32
    ) / math.sqrt(HEAD_SIZE)
    allowed = (key_pos[None, :] >= 0) & (key_pos[None, :] <= query_pos[:, None])
    attention_scores = jnp.where(allowed[None, None], attention_scores, -jnp.inf)
    row_max = jnp.max(attention_scores, axis=-1, keepdims=True)
    expd = jnp.exp(attention_scores - row_max)
    probabilities = (expd / jnp.sum(expd, axis=-1, keepdims=True)).astype(jnp.bfloat16)
    expert_mixture = jnp.einsum(
        "kyje,eku->jkyu", probabilities, value_head_tensor, preferred_element_type=jnp.float32
    )
    return expert_mixture.reshape(count, HQ * HEAD_SIZE).astype(jnp.bfloat16)


def expert_partial(gathered, w_gate, w_up, w_down):
    gate_pre = jnp.dot(gathered, w_gate, preferred_element_type=jnp.float32)
    up_pre = jnp.dot(gathered, w_up, preferred_element_type=jnp.float32)
    hidden_act = (jax.nn.silu(gate_pre) * up_pre).astype(jnp.bfloat16)
    return jnp.dot(hidden_act, w_down, preferred_element_type=jnp.float32).astype(jnp.bfloat16)


def body(
    ssm_in,
    ssm_dt,
    ssm_a,
    ssm_b,
    ssm_c,
    attn_q,
    attn_kv,
    moe_in,
    moe_routes,
    moe_prob,
    w_gate,
    w_up,
    w_down,
    *,
    seq_count,
):
    values = ssm_in.astype(jnp.float32)
    deltas = ssm_dt.astype(jnp.float32)
    local_end, local_read = sweep(values, deltas, ssm_a, ssm_b, ssm_c)
    ssm_out = ssm_correct(local_read, local_end, deltas, ssm_a, ssm_c)
    count = attn_q.shape[0]
    block_index = lax.axis_index(SEQ)
    one_back = shifted(attn_kv, SEQ, 1, seq_count)
    two_back = shifted(attn_kv, SEQ, 2, seq_count)
    window = jnp.concatenate([two_back, one_back, attn_kv], axis=0)
    first_row = block_index * count
    query_pos = first_row + jnp.arange(count, dtype=jnp.int32)
    key_pos = first_row - 2 * count + jnp.arange(3 * count, dtype=jnp.int32)
    attn_out = attend(attn_q, window, query_pos, key_pos)
    stream = (
        moe_in.astype(jnp.float32) + ssm_out.astype(jnp.float32) + attn_out.astype(jnp.float32)
    ).astype(jnp.bfloat16)
    local_tokens = stream.shape[0]
    width = stream.shape[1]
    group = seq_count // EXP_WIN
    expert_ids = jnp.arange(EXP_WIN, dtype=jnp.int32)
    matches = moe_routes[:, :, None] == expert_ids[None, None, :]
    routed = jnp.any(matches, axis=1).astype(jnp.int32)
    route_share = jnp.sum(jnp.where(matches, moe_prob[:, :, None], 0.0), axis=1)
    position_rank = jnp.cumsum(routed, axis=0) - 1
    picker = (routed[:, :, None] == 1) & (
        position_rank[:, :, None] == jnp.arange(SLOTS, dtype=jnp.int32)[None, None, :]
    )
    packed = jnp.einsum(
        "tek,td->ekd", picker.astype(jnp.bfloat16), stream, preferred_element_type=jnp.float32
    ).astype(jnp.bfloat16)
    by_expert = lax.all_to_all(packed, "eg", split_axis=0, concat_axis=0, tiled=True)
    outgoing = jnp.broadcast_to(by_expert[None], (group,) + by_expert.shape)
    arrived = lax.all_to_all(outgoing, "kg", split_axis=0, concat_axis=0, tiled=True)
    gathered = arrived.reshape(-1, width)
    partial_value = expert_partial(gathered, w_gate, w_up, w_down)
    by_source = jnp.swapaxes(partial_value.reshape(arrived.shape), 0, 1)
    returned = lax.all_to_all(
        by_source.reshape((seq_count,) + arrived.shape[2:]), SEQ, split_axis=0, concat_axis=0, tiled=True
    )
    summed = jnp.sum(returned.reshape(EXP_WIN, group, SLOTS, width), axis=1, dtype=jnp.float32)
    weighting = (picker.astype(jnp.float32) * route_share[:, :, None]).reshape(
        local_tokens, EXP_WIN * SLOTS
    )
    combined = jnp.dot(
        weighting,
        summed.reshape(EXP_WIN * SLOTS, width),
        precision=lax.Precision.HIGHEST,
        preferred_element_type=jnp.float32,
    )
    moe_out = combined.astype(jnp.bfloat16)
    return (ssm_out, attn_out, moe_out)


def solution(mesh):
    groups = mesh.shape["grp"]
    seq_count = mesh.shape["seq"]
    fine = Mesh(
        mesh.devices.reshape(groups, EXP_WIN, seq_count // EXP_WIN), ("grp",) + SEQ
    )
    rows = P(("grp",) + SEQ, None)
    return jax.shard_map(
        functools.partial(body, seq_count=seq_count),
        mesh=fine,
        in_specs=(
            rows,
            rows,
            P(),
            P(None, ("grp",) + SEQ),
            P(None, ("grp",) + SEQ),
            rows,
            rows,
            rows,
            rows,
            rows,
            P(None, SEQ),
            P(None, SEQ),
            P(SEQ, None),
        ),
        out_specs=(rows, rows, rows),
        check_vma=False,
    )
```

```python
import functools
import math

import jax
import jax.numpy as jnp
from jax import lax
from jax.experimental import pallas as pl
from jax.experimental.pallas import tpu as pltpu
from jax.sharding import Mesh, PartitionSpec as P

HQ = 32
HK = 8
HEAD_SIZE = 128
EXP_WIN = 4
CAP = 12
SLOTS = -(-CAP // 16) * 16
SEQ = ("eg", "kg")


def shifted(value, axis, by, devices):
    pairs = [(i, i + by) for i in range(devices) if 0 <= i + by < devices]
    return lax.ppermute(value, axis, pairs)


def scan_kernel(b_ref, c_ref, dt_ref, inj_ref, a_ref, read_ref, end_ref):
    states = a_ref.shape[0]
    steps = dt_ref.shape[0]
    h = [jnp.zeros(dt_ref.shape[1:], jnp.float32) for _ in range(states)]
    for t in range(steps):
        d = dt_ref[t]
        u = inj_ref[t]
        total = None
        for n in range(states):
            h[n] = jnp.exp(d * a_ref[n]) * h[n] + b_ref[n, t] * u
            term = c_ref[n, t] * h[n]
            total = term if total is None else total + term
        read_ref[t] = total
    for n in range(states):
        end_ref[n] = h[n]


def sweep(values, deltas, rates, inject_rows, read_rows):
    steps, channels = deltas.shape
    states = rates.shape[0]
    lanes = 128
    rows = channels // lanes
    tile = 8
    dt3 = deltas.reshape(steps, rows, lanes)
    inj3 = (deltas * values).reshape(steps, rows, lanes)
    a3 = rates.reshape(states, rows, lanes)
    read3, end3 = pl.pallas_call(
        scan_kernel,
        grid=(rows // tile,),
        in_specs=[
            pl.BlockSpec(memory_space=pltpu.SMEM),
            pl.BlockSpec(memory_space=pltpu.SMEM),
            pl.BlockSpec((steps, tile, lanes), lambda j: (0, j, 0)),
            pl.BlockSpec((steps, tile, lanes), lambda j: (0, j, 0)),
            pl.BlockSpec((states, tile, lanes), lambda j: (0, j, 0)),
        ],
        out_specs=[
            pl.BlockSpec((steps, tile, lanes), lambda j: (0, j, 0)),
            pl.BlockSpec((states, tile, lanes), lambda j: (0, j, 0)),
        ],
        out_shape=[
            jax.ShapeDtypeStruct((steps, rows, lanes), jnp.float32),
            jax.ShapeDtypeStruct((states, rows, lanes), jnp.float32),
        ],
    )(inject_rows, read_rows, dt3, inj3, a3)
    return end3.reshape(states, channels), read3.reshape(steps, channels)


def ssm_correct(local_read, local_end, deltas, rates, read_rows):
    mine = lax.axis_index(SEQ)
    running = jnp.cumsum(deltas, axis=0)
    ends = lax.all_gather(local_end, SEQ)
    sums = lax.all_gather(running[-1], SEQ)
    devices = sums.shape[0]
    order = jnp.arange(devices, dtype=jnp.int32)
    masked = jnp.where((order < mine)[:, None], sums, 0.0)
    after = jnp.sum(masked, axis=0)[None, :] - jnp.cumsum(masked, axis=0)
    after = jnp.maximum(after, 0.0)
    carry = jnp.exp(rates[None] * after[:, None, :]) * ends
    incoming = jnp.sum(jnp.where((order < mine)[:, None, None], carry, 0.0), axis=0)
    growth = jnp.exp(rates[None] * running[:, None, :]) * incoming[None]
    fix = jnp.sum(read_rows.T[:, :, None] * growth, axis=1)
    return (local_read + fix).astype(jnp.bfloat16)


def attend(queries, window, query_pos, key_pos):
    count = queries.shape[0]
    key_count = window.shape[0]
    repeat = HQ // HK
    query_head_tensor = queries.reshape(count, HK, repeat, HEAD_SIZE)
    key_head_tensor = window[:, : HK * HEAD_SIZE].reshape(key_count, HK, HEAD_SIZE)
    value_head_tensor = window[:, HK * HEAD_SIZE :].reshape(key_count, HK, HEAD_SIZE)
    attention_scores = jnp.einsum(
        "bajq,oaq->ajbo", query_head_tensor, key_head_tensor, preferred_element_type=jnp.float32
    ) / math.sqrt(HEAD_SIZE)
    allowed = (key_pos[None, :] >= 0) & (key_pos[None, :] <= query_pos[:, None])
    attention_scores = jnp.where(allowed[None, None], attention_scores, -jnp.inf)
    row_max = jnp.max(attention_scores, axis=-1, keepdims=True)
    expd = jnp.exp(attention_scores - row_max)
    probabilities = (expd / jnp.sum(expd, axis=-1, keepdims=True)).astype(jnp.bfloat16)
    expert_mixture = jnp.einsum(
        "kyje,eku->jkyu", probabilities, value_head_tensor, preferred_element_type=jnp.float32
    )
    return expert_mixture.reshape(count, HQ * HEAD_SIZE).astype(jnp.bfloat16)


def expert_partial(gathered, w_gate, w_up, w_down):
    gate_pre = jnp.dot(gathered, w_gate, preferred_element_type=jnp.float32)
    up_pre = jnp.dot(gathered, w_up, preferred_element_type=jnp.float32)
    hidden_act = (jax.nn.silu(gate_pre) * up_pre).astype(jnp.bfloat16)
    return jnp.dot(hidden_act, w_down, preferred_element_type=jnp.float32).astype(jnp.bfloat16)


def body(
    ssm_in,
    ssm_dt,
    ssm_a,
    ssm_b,
    ssm_c,
    attn_q,
    attn_kv,
    moe_in,
    moe_routes,
    moe_prob,
    w_gate,
    w_up,
    w_down,
    *,
    seq_count,
):
    values = ssm_in.astype(jnp.float32)
    deltas = ssm_dt.astype(jnp.float32)
    local_end, local_read = sweep(values, deltas, ssm_a, ssm_b, ssm_c)
    ssm_out = ssm_correct(local_read, local_end, deltas, ssm_a, ssm_c)
    count = attn_q.shape[0]
    block_index = lax.axis_index(SEQ)
    one_back = shifted(attn_kv, SEQ, 1, seq_count)
    two_back = shifted(attn_kv, SEQ, 2, seq_count)
    window = jnp.concatenate([two_back, one_back, attn_kv], axis=0)
    first_row = block_index * count
    query_pos = first_row + jnp.arange(count, dtype=jnp.int32)
    key_pos = first_row - 2 * count + jnp.arange(3 * count, dtype=jnp.int32)
    attn_out = attend(attn_q, window, query_pos, key_pos)
    stream = (
        moe_in.astype(jnp.float32) + ssm_out.astype(jnp.float32) + attn_out.astype(jnp.float32)
    ).astype(jnp.bfloat16)
    local_tokens = stream.shape[0]
    width = stream.shape[1]
    group = seq_count // EXP_WIN
    expert_ids = jnp.arange(EXP_WIN, dtype=jnp.int32)
    matches = moe_routes[:, :, None] == expert_ids[None, None, :]
    routed = jnp.any(matches, axis=1).astype(jnp.int32)
    route_share = jnp.sum(jnp.where(matches, moe_prob[:, :, None], 0.0), axis=1)
    position_rank = jnp.cumsum(routed, axis=0) - 1
    picker = (routed[:, :, None] == 1) & (
        position_rank[:, :, None] == jnp.arange(SLOTS, dtype=jnp.int32)[None, None, :]
    )
    packed = jnp.einsum(
        "tek,td->ekd", picker.astype(jnp.bfloat16), stream, preferred_element_type=jnp.float32
    ).astype(jnp.bfloat16)
    by_expert = lax.all_to_all(packed, "eg", split_axis=0, concat_axis=0, tiled=True)
    outgoing = jnp.broadcast_to(by_expert[None], (group,) + by_expert.shape)
    arrived = lax.all_to_all(outgoing, "kg", split_axis=0, concat_axis=0, tiled=True)
    gathered = arrived.reshape(-1, width)
    partial_value = expert_partial(gathered, w_gate, w_up, w_down)
    returned = lax.all_to_all(
        partial_value.reshape((seq_count,) + arrived.shape[2:]),
        ("kg", "eg"),
        split_axis=0,
        concat_axis=0,
        tiled=True,
    )
    summed = jnp.sum(returned.reshape(group, EXP_WIN, SLOTS, width), axis=0, dtype=jnp.float32)
    weighting = (picker.astype(jnp.float32) * route_share[:, :, None]).reshape(
        local_tokens, EXP_WIN * SLOTS
    )
    combined = jnp.dot(
        weighting,
        summed.reshape(EXP_WIN * SLOTS, width),
        precision=lax.Precision.HIGHEST,
        preferred_element_type=jnp.float32,
    )
    moe_out = combined.astype(jnp.bfloat16)
    return (ssm_out, attn_out, moe_out)


def solution(mesh):
    groups = mesh.shape["grp"]
    seq_count = mesh.shape["seq"]
    fine = Mesh(
        mesh.devices.reshape(groups, EXP_WIN, seq_count // EXP_WIN), ("grp",) + SEQ
    )
    rows = P(("grp",) + SEQ, None)
    return jax.shard_map(
        functools.partial(body, seq_count=seq_count),
        mesh=fine,
        in_specs=(
            rows,
            rows,
            P(),
            P(None, ("grp",) + SEQ),
            P(None, ("grp",) + SEQ),
            rows,
            rows,
            rows,
            rows,
            rows,
            P(None, SEQ),
            P(None, SEQ),
            P(SEQ, None),
        ),
        out_specs=(rows, rows, rows),
        check_vma=False,
    )
```

```python
import functools
import math

import jax
import jax.numpy as jnp
from jax import lax
from jax.experimental import pallas as pl
from jax.experimental.pallas import tpu as pltpu
from jax.sharding import Mesh, PartitionSpec as P

HQ = 32
HK = 8
HEAD_SIZE = 128
EXP_WIN = 4
CAP = 12
SLOTS = -(-CAP // 16) * 16
SEQ = ("eg", "kg")


def shifted(value, axis, by, devices):
    pairs = [(i, i + by) for i in range(devices) if 0 <= i + by < devices]
    return lax.ppermute(value, axis, pairs)


def scan_kernel(b_ref, c_ref, dt_ref, inj_ref, a_ref, read_ref, end_ref):
    states = a_ref.shape[0]
    steps = dt_ref.shape[0]
    h = [jnp.zeros(dt_ref.shape[1:], jnp.float32) for _ in range(states)]
    for t in range(steps):
        d = dt_ref[t]
        u = inj_ref[t]
        total = None
        for n in range(states):
            h[n] = jnp.exp(d * a_ref[n]) * h[n] + b_ref[n, t] * u
            term = c_ref[n, t] * h[n]
            total = term if total is None else total + term
        read_ref[t] = total
    for n in range(states):
        end_ref[n] = h[n]


def fix_kernel(c_ref, run_ref, read_ref, a_ref, in_ref, out_ref):
    states = a_ref.shape[0]
    for t in range(run_ref.shape[0]):
        r = run_ref[t]
        total = None
        for n in range(states):
            term = c_ref[n, t] * (jnp.exp(r * a_ref[n]) * in_ref[n])
            total = term if total is None else total + term
        out_ref[t] = read_ref[t] + total


def sweep(values, deltas, rates, inject_rows, read_rows):
    steps, channels = deltas.shape
    states = rates.shape[0]
    lanes = 128
    rows = channels // lanes
    tile = 8
    dt3 = deltas.reshape(steps, rows, lanes)
    inj3 = (deltas * values).reshape(steps, rows, lanes)
    a3 = rates.reshape(states, rows, lanes)
    read3, end3 = pl.pallas_call(
        scan_kernel,
        grid=(rows // tile,),
        in_specs=[
            pl.BlockSpec(memory_space=pltpu.SMEM),
            pl.BlockSpec(memory_space=pltpu.SMEM),
            pl.BlockSpec((steps, tile, lanes), lambda j: (0, j, 0)),
            pl.BlockSpec((steps, tile, lanes), lambda j: (0, j, 0)),
            pl.BlockSpec((states, tile, lanes), lambda j: (0, j, 0)),
        ],
        out_specs=[
            pl.BlockSpec((steps, tile, lanes), lambda j: (0, j, 0)),
            pl.BlockSpec((states, tile, lanes), lambda j: (0, j, 0)),
        ],
        out_shape=[
            jax.ShapeDtypeStruct((steps, rows, lanes), jnp.float32),
            jax.ShapeDtypeStruct((states, rows, lanes), jnp.float32),
        ],
    )(inject_rows, read_rows, dt3, inj3, a3)
    return end3.reshape(states, channels), read3


def ssm_correct(local_read, local_end, deltas, rates, read_rows):
    mine = lax.axis_index(SEQ)
    running = jnp.cumsum(deltas, axis=0)
    ends = lax.all_gather(local_end, SEQ)
    sums = lax.all_gather(running[-1], SEQ)
    devices = sums.shape[0]
    order = jnp.arange(devices, dtype=jnp.int32)
    masked = jnp.where((order < mine)[:, None], sums, 0.0)
    after = jnp.sum(masked, axis=0)[None, :] - jnp.cumsum(masked, axis=0)
    after = jnp.maximum(after, 0.0)
    carry = jnp.exp(rates[None] * after[:, None, :]) * ends
    incoming = jnp.sum(jnp.where((order < mine)[:, None, None], carry, 0.0), axis=0)
    steps, rows, lanes = local_read.shape
    states = rates.shape[0]
    tile = 8
    tiled = lambda lead: pl.BlockSpec((lead, tile, lanes), lambda j: (0, j, 0))
    out3 = pl.pallas_call(
        fix_kernel,
        grid=(rows // tile,),
        in_specs=[
            pl.BlockSpec(memory_space=pltpu.SMEM),
            tiled(steps),
            tiled(steps),
            tiled(states),
            tiled(states),
        ],
        out_specs=tiled(steps),
        out_shape=jax.ShapeDtypeStruct((steps, rows, lanes), jnp.float32),
    )(
        read_rows,
        running.reshape(steps, rows, lanes),
        local_read,
        rates.reshape(states, rows, lanes),
        incoming.reshape(states, rows, lanes),
    )
    return out3.reshape(steps, rows * lanes).astype(jnp.bfloat16)


def attend(queries, window, query_pos, key_pos):
    count = queries.shape[0]
    key_count = window.shape[0]
    repeat = HQ // HK
    query_head_tensor = queries.reshape(count, HK, repeat, HEAD_SIZE)
    key_head_tensor = window[:, : HK * HEAD_SIZE].reshape(key_count, HK, HEAD_SIZE)
    value_head_tensor = window[:, HK * HEAD_SIZE :].reshape(key_count, HK, HEAD_SIZE)
    attention_scores = jnp.einsum(
        "bajq,oaq->ajbo", query_head_tensor, key_head_tensor, preferred_element_type=jnp.float32
    ) / math.sqrt(HEAD_SIZE)
    allowed = (key_pos[None, :] >= 0) & (key_pos[None, :] <= query_pos[:, None])
    attention_scores = jnp.where(allowed[None, None], attention_scores, -jnp.inf)
    row_max = jnp.max(attention_scores, axis=-1, keepdims=True)
    expd = jnp.exp(attention_scores - row_max)
    probabilities = (expd / jnp.sum(expd, axis=-1, keepdims=True)).astype(jnp.bfloat16)
    expert_mixture = jnp.einsum(
        "kyje,eku->jkyu", probabilities, value_head_tensor, preferred_element_type=jnp.float32
    )
    return expert_mixture.reshape(count, HQ * HEAD_SIZE).astype(jnp.bfloat16)


def expert_partial(gathered, w_gate, w_up, w_down):
    gate_pre = jnp.dot(gathered, w_gate, preferred_element_type=jnp.float32)
    up_pre = jnp.dot(gathered, w_up, preferred_element_type=jnp.float32)
    hidden_act = (jax.nn.silu(gate_pre) * up_pre).astype(jnp.bfloat16)
    return jnp.dot(hidden_act, w_down, preferred_element_type=jnp.float32).astype(jnp.bfloat16)


def body(
    ssm_in,
    ssm_dt,
    ssm_a,
    ssm_b,
    ssm_c,
    attn_q,
    attn_kv,
    moe_in,
    moe_routes,
    moe_prob,
    w_gate,
    w_up,
    w_down,
    *,
    seq_count,
):
    values = ssm_in.astype(jnp.float32)
    deltas = ssm_dt.astype(jnp.float32)
    local_end, local_read = sweep(values, deltas, ssm_a, ssm_b, ssm_c)
    ssm_out = ssm_correct(local_read, local_end, deltas, ssm_a, ssm_c)
    count = attn_q.shape[0]
    block_index = lax.axis_index(SEQ)
    one_back = shifted(attn_kv, SEQ, 1, seq_count)
    two_back = shifted(attn_kv, SEQ, 2, seq_count)
    window = jnp.concatenate([two_back, one_back, attn_kv], axis=0)
    first_row = block_index * count
    query_pos = first_row + jnp.arange(count, dtype=jnp.int32)
    key_pos = first_row - 2 * count + jnp.arange(3 * count, dtype=jnp.int32)
    attn_out = attend(attn_q, window, query_pos, key_pos)
    stream = (
        moe_in.astype(jnp.float32) + ssm_out.astype(jnp.float32) + attn_out.astype(jnp.float32)
    ).astype(jnp.bfloat16)
    local_tokens = stream.shape[0]
    width = stream.shape[1]
    group = seq_count // EXP_WIN
    expert_ids = jnp.arange(EXP_WIN, dtype=jnp.int32)
    matches = moe_routes[:, :, None] == expert_ids[None, None, :]
    routed = jnp.any(matches, axis=1).astype(jnp.int32)
    route_share = jnp.sum(jnp.where(matches, moe_prob[:, :, None], 0.0), axis=1)
    position_rank = jnp.cumsum(routed, axis=0) - 1
    picker = (routed[:, :, None] == 1) & (
        position_rank[:, :, None] == jnp.arange(SLOTS, dtype=jnp.int32)[None, None, :]
    )
    packed = jnp.einsum(
        "tek,td->ekd", picker.astype(jnp.bfloat16), stream, preferred_element_type=jnp.float32
    ).astype(jnp.bfloat16)
    by_expert = lax.all_to_all(packed, "eg", split_axis=0, concat_axis=0, tiled=True)
    outgoing = jnp.broadcast_to(by_expert[None], (group,) + by_expert.shape)
    arrived = lax.all_to_all(outgoing, "kg", split_axis=0, concat_axis=0, tiled=True)
    gathered = arrived.reshape(-1, width)
    partial_value = expert_partial(gathered, w_gate, w_up, w_down)
    by_source = jnp.swapaxes(partial_value.reshape(arrived.shape), 0, 1)
    returned = lax.all_to_all(
        by_source.reshape((seq_count,) + arrived.shape[2:]), SEQ, split_axis=0, concat_axis=0, tiled=True
    )
    summed = jnp.sum(returned.reshape(EXP_WIN, group, SLOTS, width), axis=1, dtype=jnp.float32)
    weighting = (picker.astype(jnp.float32) * route_share[:, :, None]).reshape(
        local_tokens, EXP_WIN * SLOTS
    )
    combined = jnp.dot(
        weighting,
        summed.reshape(EXP_WIN * SLOTS, width),
        precision=lax.Precision.HIGHEST,
        preferred_element_type=jnp.float32,
    )
    moe_out = combined.astype(jnp.bfloat16)
    return (ssm_out, attn_out, moe_out)


def solution(mesh):
    groups = mesh.shape["grp"]
    seq_count = mesh.shape["seq"]
    fine = Mesh(
        mesh.devices.reshape(groups, EXP_WIN, seq_count // EXP_WIN), ("grp",) + SEQ
    )
    rows = P(("grp",) + SEQ, None)
    return jax.shard_map(
        functools.partial(body, seq_count=seq_count),
        mesh=fine,
        in_specs=(
            rows,
            rows,
            P(),
            P(None, ("grp",) + SEQ),
            P(None, ("grp",) + SEQ),
            rows,
            rows,
            rows,
            rows,
            rows,
            P(None, SEQ),
            P(None, SEQ),
            P(SEQ, None),
        ),
        out_specs=(rows, rows, rows),
        check_vma=False,
    )
```

```python
import functools
import math

import jax
import jax.numpy as jnp
from jax import lax
from jax.experimental import pallas as pl
from jax.experimental.pallas import tpu as pltpu
from jax.sharding import Mesh, PartitionSpec as P

HQ = 32
HK = 8
HEAD_SIZE = 128
EXP_WIN = 4
CAP = 12
SLOTS = -(-CAP // 16) * 16
SEQ = ("eg", "kg")


def shifted(value, axis, by, devices):
    pairs = [(i, i + by) for i in range(devices) if 0 <= i + by < devices]
    return lax.ppermute(value, axis, pairs)


def scan_kernel(b_ref, c_ref, dt_ref, inj_ref, a_ref, read_ref, end_ref):
    states = a_ref.shape[0]
    steps = dt_ref.shape[0]
    h = [jnp.zeros(dt_ref.shape[1:], jnp.float32) for _ in range(states)]
    for t in range(steps):
        d = dt_ref[t]
        u = inj_ref[t]
        total = None
        for n in range(states):
            h[n] = jnp.exp(d * a_ref[n]) * h[n] + b_ref[n, t] * u
            term = c_ref[n, t] * h[n]
            total = term if total is None else total + term
        read_ref[t] = total
    for n in range(states):
        end_ref[n] = h[n]


def sweep(values, deltas, rates, inject_rows, read_rows):
    steps, channels = deltas.shape
    states = rates.shape[0]
    lanes = 128
    rows = channels // lanes
    tile = 8
    dt3 = deltas.reshape(steps, rows, lanes)
    inj3 = (deltas * values).reshape(steps, rows, lanes)
    a3 = rates.reshape(states, rows, lanes)
    read3, end3 = pl.pallas_call(
        scan_kernel,
        grid=(rows // tile,),
        in_specs=[
            pl.BlockSpec(memory_space=pltpu.SMEM),
            pl.BlockSpec(memory_space=pltpu.SMEM),
            pl.BlockSpec((steps, tile, lanes), lambda j: (0, j, 0)),
            pl.BlockSpec((steps, tile, lanes), lambda j: (0, j, 0)),
            pl.BlockSpec((states, tile, lanes), lambda j: (0, j, 0)),
        ],
        out_specs=[
            pl.BlockSpec((steps, tile, lanes), lambda j: (0, j, 0)),
            pl.BlockSpec((states, tile, lanes), lambda j: (0, j, 0)),
        ],
        out_shape=[
            jax.ShapeDtypeStruct((steps, rows, lanes), jnp.float32),
            jax.ShapeDtypeStruct((states, rows, lanes), jnp.float32),
        ],
    )(inject_rows, read_rows, dt3, inj3, a3)
    return end3.reshape(states, channels), read3.reshape(steps, channels)


def ssm_correct(local_read, local_end, deltas, rates, read_rows):
    mine = lax.axis_index(SEQ)
    running = jnp.cumsum(deltas, axis=0)
    ends = lax.all_gather(local_end, SEQ)
    sums = lax.all_gather(running[-1], SEQ)
    devices = sums.shape[0]
    order = jnp.arange(devices, dtype=jnp.int32)
    masked = jnp.where((order < mine)[:, None], sums, 0.0)
    after = jnp.sum(masked, axis=0)[None, :] - jnp.cumsum(masked, axis=0)
    after = jnp.maximum(after, 0.0)
    carry = jnp.exp(rates[None] * after[:, None, :]) * ends
    incoming = jnp.sum(jnp.where((order < mine)[:, None, None], carry, 0.0), axis=0)
    growth = jnp.exp(rates[None] * running[:, None, :]) * incoming[None]
    fix = jnp.sum(read_rows.T[:, :, None] * growth, axis=1)
    return (local_read + fix).astype(jnp.bfloat16)


def attend(queries, window, query_pos, key_pos):
    count = queries.shape[0]
    key_count = window.shape[0]
    repeat = HQ // HK
    query_head_tensor = queries.reshape(count, HK, repeat, HEAD_SIZE)
    key_head_tensor = window[:, : HK * HEAD_SIZE].reshape(key_count, HK, HEAD_SIZE)
    value_head_tensor = window[:, HK * HEAD_SIZE :].reshape(key_count, HK, HEAD_SIZE)
    attention_scores = jnp.einsum(
        "bajq,oaq->ajbo", query_head_tensor, key_head_tensor, preferred_element_type=jnp.float32
    ) / math.sqrt(HEAD_SIZE)
    allowed = (key_pos[None, :] >= 0) & (key_pos[None, :] <= query_pos[:, None])
    attention_scores = jnp.where(allowed[None, None], attention_scores, -jnp.inf)
    row_max = jnp.max(attention_scores, axis=-1, keepdims=True)
    expd = jnp.exp(attention_scores - row_max)
    probabilities = (expd / jnp.sum(expd, axis=-1, keepdims=True)).astype(jnp.bfloat16)
    expert_mixture = jnp.einsum(
        "kyje,eku->jkyu", probabilities, value_head_tensor, preferred_element_type=jnp.float32
    )
    return expert_mixture.reshape(count, HQ * HEAD_SIZE).astype(jnp.bfloat16)


def expert_partial(gathered, w_gate, w_up, w_down):
    gate_pre = jnp.dot(gathered, w_gate, preferred_element_type=jnp.float32)
    up_pre = jnp.dot(gathered, w_up, preferred_element_type=jnp.float32)
    hidden_act = (jax.nn.silu(gate_pre) * up_pre).astype(jnp.bfloat16)
    return jnp.dot(hidden_act, w_down, preferred_element_type=jnp.float32).astype(jnp.bfloat16)


def body(
    ssm_in,
    ssm_dt,
    ssm_a,
    ssm_b,
    ssm_c,
    attn_q,
    attn_kv,
    moe_in,
    moe_routes,
    moe_prob,
    w_gate,
    w_up,
    w_down,
    *,
    seq_count,
):
    values = ssm_in.astype(jnp.float32)
    deltas = ssm_dt.astype(jnp.float32)
    local_end, local_read = sweep(values, deltas, ssm_a, ssm_b, ssm_c)
    ssm_out = ssm_correct(local_read, local_end, deltas, ssm_a, ssm_c)
    count = attn_q.shape[0]
    block_index = lax.axis_index(SEQ)
    one_back = shifted(attn_kv, SEQ, 1, seq_count)
    two_back = shifted(attn_kv, SEQ, 2, seq_count)
    window = jnp.concatenate([two_back, one_back, attn_kv], axis=0)
    first_row = block_index * count
    query_pos = first_row + jnp.arange(count, dtype=jnp.int32)
    key_pos = first_row - 2 * count + jnp.arange(3 * count, dtype=jnp.int32)
    attn_out = attend(attn_q, window, query_pos, key_pos)
    stream = (
        moe_in.astype(jnp.float32) + ssm_out.astype(jnp.float32) + attn_out.astype(jnp.float32)
    ).astype(jnp.bfloat16)
    local_tokens = stream.shape[0]
    width = stream.shape[1]
    group = seq_count // EXP_WIN
    expert_ids = jnp.arange(EXP_WIN, dtype=jnp.int32)
    matches = moe_routes[:, :, None] == expert_ids[None, None, :]
    routed = jnp.any(matches, axis=1).astype(jnp.int32)
    route_share = jnp.sum(jnp.where(matches, moe_prob[:, :, None], 0.0), axis=1)
    position_rank = jnp.cumsum(routed, axis=0) - 1
    picker = (routed[:, :, None] == 1) & (
        position_rank[:, :, None] == jnp.arange(SLOTS, dtype=jnp.int32)[None, None, :]
    )
    packed = jnp.einsum(
        "tek,td->ekd", picker.astype(jnp.bfloat16), stream, preferred_element_type=jnp.float32
    ).astype(jnp.bfloat16)
    by_expert = lax.all_to_all(packed, "eg", split_axis=0, concat_axis=0, tiled=True)
    pieces = [by_expert]
    for by in range(1, group):
        pairs = [(i, (i + by) % group) for i in range(group)]
        pieces.append(lax.ppermute(by_expert, "kg", pairs))
    mine = lax.axis_index("kg")
    arrived = jnp.take(jnp.stack(pieces), (mine - jnp.arange(group)) % group, axis=0)
    gathered = arrived.reshape(-1, width)
    partial_value = expert_partial(gathered, w_gate, w_up, w_down)
    returned = lax.all_to_all(
        partial_value.reshape((seq_count,) + arrived.shape[2:]),
        ("kg", "eg"),
        split_axis=0,
        concat_axis=0,
        tiled=True,
    )
    summed = jnp.sum(returned.reshape(group, EXP_WIN, SLOTS, width), axis=0, dtype=jnp.float32)
    weighting = (picker.astype(jnp.float32) * route_share[:, :, None]).reshape(
        local_tokens, EXP_WIN * SLOTS
    )
    combined = jnp.dot(
        weighting,
        summed.reshape(EXP_WIN * SLOTS, width),
        precision=lax.Precision.HIGHEST,
        preferred_element_type=jnp.float32,
    )
    moe_out = combined.astype(jnp.bfloat16)
    return (ssm_out, attn_out, moe_out)


def solution(mesh):
    groups = mesh.shape["grp"]
    seq_count = mesh.shape["seq"]
    fine = Mesh(
        mesh.devices.reshape(groups, EXP_WIN, seq_count // EXP_WIN), ("grp",) + SEQ
    )
    rows = P(("grp",) + SEQ, None)
    return jax.shard_map(
        functools.partial(body, seq_count=seq_count),
        mesh=fine,
        in_specs=(
            rows,
            rows,
            P(),
            P(None, ("grp",) + SEQ),
            P(None, ("grp",) + SEQ),
            rows,
            rows,
            rows,
            rows,
            rows,
            P(None, SEQ),
            P(None, SEQ),
            P(SEQ, None),
        ),
        out_specs=(rows, rows, rows),
        check_vma=False,
    )
```

```python
import functools
import math

import jax
import jax.numpy as jnp
from jax import lax
from jax.experimental import pallas as pl
from jax.experimental.pallas import tpu as pltpu
from jax.sharding import Mesh, PartitionSpec as P

HQ = 32
HK = 8
HEAD_SIZE = 128
EXP_WIN = 4
CAP = 12
SLOTS = -(-CAP // 16) * 16
SEQ = ("eg", "kg")


def shifted(value, axis, by, devices):
    pairs = [(i, i + by) for i in range(devices) if 0 <= i + by < devices]
    return lax.ppermute(value, axis, pairs)


def scan_kernel(b_ref, c_ref, dt_ref, inj_ref, a_ref, read_ref, end_ref):
    states = a_ref.shape[0]
    steps = dt_ref.shape[0]
    h = [jnp.zeros(dt_ref.shape[1:], jnp.float32) for _ in range(states)]
    for t in range(steps):
        d = dt_ref[t]
        u = inj_ref[t]
        total = None
        for n in range(states):
            h[n] = jnp.exp(d * a_ref[n]) * h[n] + b_ref[n, t] * u
            term = c_ref[n, t] * h[n]
            total = term if total is None else total + term
        read_ref[t] = total
    for n in range(states):
        end_ref[n] = h[n]


def sweep(values, deltas, rates, inject_rows, read_rows):
    steps, channels = deltas.shape
    states = rates.shape[0]
    lanes = 128
    rows = channels // lanes
    tile = 8
    dt3 = deltas.reshape(steps, rows, lanes)
    inj3 = (deltas * values).reshape(steps, rows, lanes)
    a3 = rates.reshape(states, rows, lanes)
    read3, end3 = pl.pallas_call(
        scan_kernel,
        grid=(rows // tile,),
        in_specs=[
            pl.BlockSpec(memory_space=pltpu.SMEM),
            pl.BlockSpec(memory_space=pltpu.SMEM),
            pl.BlockSpec((steps, tile, lanes), lambda j: (0, j, 0)),
            pl.BlockSpec((steps, tile, lanes), lambda j: (0, j, 0)),
            pl.BlockSpec((states, tile, lanes), lambda j: (0, j, 0)),
        ],
        out_specs=[
            pl.BlockSpec((steps, tile, lanes), lambda j: (0, j, 0)),
            pl.BlockSpec((states, tile, lanes), lambda j: (0, j, 0)),
        ],
        out_shape=[
            jax.ShapeDtypeStruct((steps, rows, lanes), jnp.float32),
            jax.ShapeDtypeStruct((states, rows, lanes), jnp.float32),
        ],
    )(inject_rows, read_rows, dt3, inj3, a3)
    return end3.reshape(states, channels), read3.reshape(steps, channels)


def ssm_correct(local_read, local_end, deltas, rates, read_rows):
    mine = lax.axis_index(SEQ)
    running = jnp.cumsum(deltas, axis=0)
    ends = lax.all_gather(local_end, SEQ)
    sums = lax.all_gather(running[-1], SEQ)
    devices = sums.shape[0]
    order = jnp.arange(devices, dtype=jnp.int32)
    masked = jnp.where((order < mine)[:, None], sums, 0.0)
    after = jnp.sum(masked, axis=0)[None, :] - jnp.cumsum(masked, axis=0)
    after = jnp.maximum(after, 0.0)
    carry = jnp.exp(rates[None] * after[:, None, :]) * ends
    incoming = jnp.sum(jnp.where((order < mine)[:, None, None], carry, 0.0), axis=0)
    growth = jnp.exp(rates[None] * running[:, None, :]) * incoming[None]
    fix = jnp.sum(read_rows.T[:, :, None] * growth, axis=1)
    return (local_read + fix).astype(jnp.bfloat16)


def attend(queries, window, query_pos, key_pos):
    count = queries.shape[0]
    key_count = window.shape[0]
    repeat = HQ // HK
    query_head_tensor = queries.reshape(count, HK, repeat, HEAD_SIZE)
    key_head_tensor = window[:, : HK * HEAD_SIZE].reshape(key_count, HK, HEAD_SIZE)
    value_head_tensor = window[:, HK * HEAD_SIZE :].reshape(key_count, HK, HEAD_SIZE)
    attention_scores = jnp.einsum(
        "bajq,oaq->ajbo", query_head_tensor, key_head_tensor, preferred_element_type=jnp.float32
    ) / math.sqrt(HEAD_SIZE)
    allowed = (key_pos[None, :] >= 0) & (key_pos[None, :] <= query_pos[:, None])
    attention_scores = jnp.where(allowed[None, None], attention_scores, -jnp.inf)
    row_max = jnp.max(attention_scores, axis=-1, keepdims=True)
    expd = jnp.exp(attention_scores - row_max)
    probabilities = (expd / jnp.sum(expd, axis=-1, keepdims=True)).astype(jnp.bfloat16)
    expert_mixture = jnp.einsum(
        "kyje,eku->jkyu", probabilities, value_head_tensor, preferred_element_type=jnp.float32
    )
    return expert_mixture.reshape(count, HQ * HEAD_SIZE).astype(jnp.bfloat16)


def expert_partial(gathered, w_gate, w_up, w_down):
    gate_pre = jnp.dot(gathered, w_gate, preferred_element_type=jnp.float32)
    up_pre = jnp.dot(gathered, w_up, preferred_element_type=jnp.float32)
    hidden_act = (jax.nn.silu(gate_pre) * up_pre).astype(jnp.bfloat16)
    return jnp.dot(hidden_act, w_down, preferred_element_type=jnp.float32).astype(jnp.bfloat16)


def body(
    ssm_in,
    ssm_dt,
    ssm_a,
    ssm_b,
    ssm_c,
    attn_q,
    attn_kv,
    moe_in,
    moe_routes,
    moe_prob,
    w_gate,
    w_up,
    w_down,
    *,
    seq_count,
):
    values = ssm_in.astype(jnp.float32)
    deltas = ssm_dt.astype(jnp.float32)
    local_end, local_read = sweep(values, deltas, ssm_a, ssm_b, ssm_c)
    ssm_out = ssm_correct(local_read, local_end, deltas, ssm_a, ssm_c)
    count = attn_q.shape[0]
    block_index = lax.axis_index(SEQ)
    one_back = shifted(attn_kv, SEQ, 1, seq_count)
    two_back = shifted(attn_kv, SEQ, 2, seq_count)
    window = jnp.concatenate([two_back, one_back, attn_kv], axis=0)
    first_row = block_index * count
    query_pos = first_row + jnp.arange(count, dtype=jnp.int32)
    key_pos = first_row - 2 * count + jnp.arange(3 * count, dtype=jnp.int32)
    attn_out = attend(attn_q, window, query_pos, key_pos)
    stream = (
        moe_in.astype(jnp.float32) + ssm_out.astype(jnp.float32) + attn_out.astype(jnp.float32)
    ).astype(jnp.bfloat16)
    local_tokens = stream.shape[0]
    width = stream.shape[1]
    group = seq_count // EXP_WIN
    expert_ids = jnp.arange(EXP_WIN, dtype=jnp.int32)
    matches = moe_routes[:, :, None] == expert_ids[None, None, :]
    routed = jnp.any(matches, axis=1).astype(jnp.int32)
    route_share = jnp.sum(jnp.where(matches, moe_prob[:, :, None], 0.0), axis=1)
    position_rank = jnp.cumsum(routed, axis=0) - 1
    picker = (routed[:, :, None] == 1) & (
        position_rank[:, :, None] == jnp.arange(SLOTS, dtype=jnp.int32)[None, None, :]
    )
    packed = jnp.einsum(
        "tek,td->ekd", picker.astype(jnp.bfloat16), stream, preferred_element_type=jnp.float32
    ).astype(jnp.bfloat16)
    by_expert = lax.all_to_all(packed, "eg", split_axis=0, concat_axis=0, tiled=True)
    outgoing = jnp.broadcast_to(by_expert[:, None], (EXP_WIN, group) + by_expert.shape[1:])
    arrived = lax.all_to_all(outgoing, "kg", split_axis=1, concat_axis=1, tiled=True)
    gathered = arrived.reshape(-1, width)
    partial_value = expert_partial(gathered, w_gate, w_up, w_down)
    returned = lax.all_to_all(
        partial_value.reshape((seq_count,) + arrived.shape[2:]), SEQ, split_axis=0, concat_axis=0, tiled=True
    )
    summed = jnp.sum(returned.reshape(EXP_WIN, group, SLOTS, width), axis=1, dtype=jnp.float32)
    weighting = (picker.astype(jnp.float32) * route_share[:, :, None]).reshape(
        local_tokens, EXP_WIN * SLOTS
    )
    combined = jnp.dot(
        weighting,
        summed.reshape(EXP_WIN * SLOTS, width),
        precision=lax.Precision.HIGHEST,
        preferred_element_type=jnp.float32,
    )
    moe_out = combined.astype(jnp.bfloat16)
    return (ssm_out, attn_out, moe_out)


def solution(mesh):
    groups = mesh.shape["grp"]
    seq_count = mesh.shape["seq"]
    fine = Mesh(
        mesh.devices.reshape(groups, EXP_WIN, seq_count // EXP_WIN), ("grp",) + SEQ
    )
    rows = P(("grp",) + SEQ, None)
    return jax.shard_map(
        functools.partial(body, seq_count=seq_count),
        mesh=fine,
        in_specs=(
            rows,
            rows,
            P(),
            P(None, ("grp",) + SEQ),
            P(None, ("grp",) + SEQ),
            rows,
            rows,
            rows,
            rows,
            rows,
            P(None, SEQ),
            P(None, SEQ),
            P(SEQ, None),
        ),
        out_specs=(rows, rows, rows),
        check_vma=False,
    )
```

```python
import functools
import math

import jax
import jax.numpy as jnp
from jax import lax
from jax.experimental import pallas as pl
from jax.experimental.pallas import tpu as pltpu
from jax.sharding import Mesh, PartitionSpec as P

HQ = 32
HK = 8
HEAD_SIZE = 128
EXP_WIN = 4
CAP = 12
SLOTS = -(-CAP // 16) * 16
SEQ = ("eg", "kg")


def shifted(value, axis, by, devices):
    pairs = [(i, i + by) for i in range(devices) if 0 <= i + by < devices]
    return lax.ppermute(value, axis, pairs)


def scan_kernel(b_ref, c_ref, dt_ref, inj_ref, a_ref, read_ref, end_ref):
    states = a_ref.shape[0]
    steps = dt_ref.shape[0]
    h = [jnp.zeros(dt_ref.shape[1:], jnp.float32) for _ in range(states)]
    for t in range(steps):
        d = dt_ref[t]
        u = inj_ref[t]
        total = None
        for n in range(states):
            h[n] = jnp.exp(d * a_ref[n]) * h[n] + b_ref[n, t] * u
            term = c_ref[n, t] * h[n]
            total = term if total is None else total + term
        read_ref[t] = total
    for n in range(states):
        end_ref[n] = h[n]


def sweep(values, deltas, rates, inject_rows, read_rows):
    steps, channels = deltas.shape
    states = rates.shape[0]
    lanes = 128
    rows = channels // lanes
    tile = 8
    dt3 = deltas.reshape(steps, rows, lanes)
    inj3 = (deltas * values).reshape(steps, rows, lanes)
    a3 = rates.reshape(states, rows, lanes)
    read3, end3 = pl.pallas_call(
        scan_kernel,
        grid=(rows // tile,),
        in_specs=[
            pl.BlockSpec(memory_space=pltpu.SMEM),
            pl.BlockSpec(memory_space=pltpu.SMEM),
            pl.BlockSpec((steps, tile, lanes), lambda j: (0, j, 0)),
            pl.BlockSpec((steps, tile, lanes), lambda j: (0, j, 0)),
            pl.BlockSpec((states, tile, lanes), lambda j: (0, j, 0)),
        ],
        out_specs=[
            pl.BlockSpec((steps, tile, lanes), lambda j: (0, j, 0)),
            pl.BlockSpec((states, tile, lanes), lambda j: (0, j, 0)),
        ],
        out_shape=[
            jax.ShapeDtypeStruct((steps, rows, lanes), jnp.float32),
            jax.ShapeDtypeStruct((states, rows, lanes), jnp.float32),
        ],
    )(inject_rows, read_rows, dt3, inj3, a3)
    return end3.reshape(states, channels), read3.reshape(steps, channels)


def ssm_correct(local_read, local_end, deltas, rates, read_rows):
    mine = lax.axis_index(SEQ)
    running = jnp.cumsum(deltas, axis=0)
    ends = lax.all_gather(local_end, SEQ)
    sums = lax.all_gather(running[-1], SEQ)
    devices = sums.shape[0]
    order = jnp.arange(devices, dtype=jnp.int32)
    masked = jnp.where((order < mine)[:, None], sums, 0.0)
    after = jnp.sum(masked, axis=0)[None, :] - jnp.cumsum(masked, axis=0)
    after = jnp.maximum(after, 0.0)
    through = jnp.where((order < mine)[:, None, None], jnp.exp(rates[None] * after[:, None, :]), 0.0)
    growth = read_rows.T[:, :, None] * jnp.exp(rates[None] * running[:, None, :])
    through, growth = lax.optimization_barrier((through, growth))
    incoming = jnp.sum(through * ends, axis=0)
    fix = jnp.sum(growth * incoming[None], axis=1)
    return (local_read + fix).astype(jnp.bfloat16)


def attend(queries, window, query_pos, key_pos):
    count = queries.shape[0]
    key_count = window.shape[0]
    repeat = HQ // HK
    query_head_tensor = queries.reshape(count, HK, repeat, HEAD_SIZE)
    key_head_tensor = window[:, : HK * HEAD_SIZE].reshape(key_count, HK, HEAD_SIZE)
    value_head_tensor = window[:, HK * HEAD_SIZE :].reshape(key_count, HK, HEAD_SIZE)
    attention_scores = jnp.einsum(
        "bajq,oaq->ajbo", query_head_tensor, key_head_tensor, preferred_element_type=jnp.float32
    ) / math.sqrt(HEAD_SIZE)
    allowed = (key_pos[None, :] >= 0) & (key_pos[None, :] <= query_pos[:, None])
    attention_scores = jnp.where(allowed[None, None], attention_scores, -jnp.inf)
    row_max = jnp.max(attention_scores, axis=-1, keepdims=True)
    expd = jnp.exp(attention_scores - row_max)
    probabilities = (expd / jnp.sum(expd, axis=-1, keepdims=True)).astype(jnp.bfloat16)
    expert_mixture = jnp.einsum(
        "kyje,eku->jkyu", probabilities, value_head_tensor, preferred_element_type=jnp.float32
    )
    return expert_mixture.reshape(count, HQ * HEAD_SIZE).astype(jnp.bfloat16)


def expert_partial(gathered, w_gate, w_up, w_down):
    gate_pre = jnp.dot(gathered, w_gate, preferred_element_type=jnp.float32)
    up_pre = jnp.dot(gathered, w_up, preferred_element_type=jnp.float32)
    hidden_act = (jax.nn.silu(gate_pre) * up_pre).astype(jnp.bfloat16)
    return jnp.dot(hidden_act, w_down, preferred_element_type=jnp.float32).astype(jnp.bfloat16)


def body(
    ssm_in,
    ssm_dt,
    ssm_a,
    ssm_b,
    ssm_c,
    attn_q,
    attn_kv,
    moe_in,
    moe_routes,
    moe_prob,
    w_gate,
    w_up,
    w_down,
    *,
    seq_count,
):
    values = ssm_in.astype(jnp.float32)
    deltas = ssm_dt.astype(jnp.float32)
    local_end, local_read = sweep(values, deltas, ssm_a, ssm_b, ssm_c)
    ssm_out = ssm_correct(local_read, local_end, deltas, ssm_a, ssm_c)
    count = attn_q.shape[0]
    block_index = lax.axis_index(SEQ)
    one_back = shifted(attn_kv, SEQ, 1, seq_count)
    two_back = shifted(attn_kv, SEQ, 2, seq_count)
    window = jnp.concatenate([two_back, one_back, attn_kv], axis=0)
    first_row = block_index * count
    query_pos = first_row + jnp.arange(count, dtype=jnp.int32)
    key_pos = first_row - 2 * count + jnp.arange(3 * count, dtype=jnp.int32)
    attn_out = attend(attn_q, window, query_pos, key_pos)
    stream = (
        moe_in.astype(jnp.float32) + ssm_out.astype(jnp.float32) + attn_out.astype(jnp.float32)
    ).astype(jnp.bfloat16)
    local_tokens = stream.shape[0]
    width = stream.shape[1]
    group = seq_count // EXP_WIN
    expert_ids = jnp.arange(EXP_WIN, dtype=jnp.int32)
    matches = moe_routes[:, :, None] == expert_ids[None, None, :]
    routed = jnp.any(matches, axis=1).astype(jnp.int32)
    route_share = jnp.sum(jnp.where(matches, moe_prob[:, :, None], 0.0), axis=1)
    position_rank = jnp.cumsum(routed, axis=0) - 1
    picker = (routed[:, :, None] == 1) & (
        position_rank[:, :, None] == jnp.arange(SLOTS, dtype=jnp.int32)[None, None, :]
    )
    packed = jnp.einsum(
        "tek,td->ekd", picker.astype(jnp.bfloat16), stream, preferred_element_type=jnp.float32
    ).astype(jnp.bfloat16)
    by_expert = lax.all_to_all(packed, "eg", split_axis=0, concat_axis=0, tiled=True)
    outgoing = jnp.broadcast_to(by_expert[:, None], (EXP_WIN, group) + by_expert.shape[1:])
    arrived = lax.all_to_all(outgoing, "kg", split_axis=1, concat_axis=1, tiled=True)
    gathered = arrived.reshape(-1, width)
    partial_value = expert_partial(gathered, w_gate, w_up, w_down)
    returned = lax.all_to_all(
        partial_value.reshape((seq_count,) + arrived.shape[2:]), SEQ, split_axis=0, concat_axis=0, tiled=True
    )
    summed = jnp.sum(returned.reshape(EXP_WIN, group, SLOTS, width), axis=1, dtype=jnp.float32)
    weighting = (picker.astype(jnp.float32) * route_share[:, :, None]).reshape(
        local_tokens, EXP_WIN * SLOTS
    )
    combined = jnp.dot(
        weighting,
        summed.reshape(EXP_WIN * SLOTS, width),
        precision=lax.Precision.HIGHEST,
        preferred_element_type=jnp.float32,
    )
    moe_out = combined.astype(jnp.bfloat16)
    return (ssm_out, attn_out, moe_out)


def solution(mesh):
    groups = mesh.shape["grp"]
    seq_count = mesh.shape["seq"]
    fine = Mesh(
        mesh.devices.reshape(groups, EXP_WIN, seq_count // EXP_WIN), ("grp",) + SEQ
    )
    rows = P(("grp",) + SEQ, None)
    return jax.shard_map(
        functools.partial(body, seq_count=seq_count),
        mesh=fine,
        in_specs=(
            rows,
            rows,
            P(),
            P(None, ("grp",) + SEQ),
            P(None, ("grp",) + SEQ),
            rows,
            rows,
            rows,
            rows,
            rows,
            P(None, SEQ),
            P(None, SEQ),
            P(SEQ, None),
        ),
        out_specs=(rows, rows, rows),
        check_vma=False,
    )
```

```python
import functools
import math

import jax
import jax.numpy as jnp
from jax import lax
from jax.experimental import pallas as pl
from jax.experimental.pallas import tpu as pltpu
from jax.sharding import Mesh, PartitionSpec as P

HQ = 32
HK = 8
HEAD_SIZE = 128
EXP_WIN = 4
CAP = 12
SLOTS = -(-CAP // 16) * 16
SEQ = ("eg", "kg")


def shifted(value, axis, by, devices):
    pairs = [(i, i + by) for i in range(devices) if 0 <= i + by < devices]
    return lax.ppermute(value, axis, pairs)


def scan_kernel(b_ref, c_ref, dt_ref, inj_ref, a_ref, read_ref, end_ref):
    states = a_ref.shape[0]
    steps = dt_ref.shape[0]
    h = [jnp.zeros(dt_ref.shape[1:], jnp.float32) for _ in range(states)]
    for t in range(steps):
        d = dt_ref[t]
        u = inj_ref[t]
        total = None
        for n in range(states):
            h[n] = jnp.exp(d * a_ref[n]) * h[n] + b_ref[n, t] * u
            term = c_ref[n, t] * h[n]
            total = term if total is None else total + term
        read_ref[t] = total
    for n in range(states):
        end_ref[n] = h[n]


def sweep(values, deltas, rates, inject_rows, read_rows):
    steps, channels = deltas.shape
    states = rates.shape[0]
    lanes = 128
    rows = channels // lanes
    tile = 8
    dt3 = deltas.reshape(steps, rows, lanes)
    inj3 = (deltas * values).reshape(steps, rows, lanes)
    a3 = rates.reshape(states, rows, lanes)
    read3, end3 = pl.pallas_call(
        scan_kernel,
        grid=(rows // tile,),
        in_specs=[
            pl.BlockSpec(memory_space=pltpu.SMEM),
            pl.BlockSpec(memory_space=pltpu.SMEM),
            pl.BlockSpec((steps, tile, lanes), lambda j: (0, j, 0)),
            pl.BlockSpec((steps, tile, lanes), lambda j: (0, j, 0)),
            pl.BlockSpec((states, tile, lanes), lambda j: (0, j, 0)),
        ],
        out_specs=[
            pl.BlockSpec((steps, tile, lanes), lambda j: (0, j, 0)),
            pl.BlockSpec((states, tile, lanes), lambda j: (0, j, 0)),
        ],
        out_shape=[
            jax.ShapeDtypeStruct((steps, rows, lanes), jnp.float32),
            jax.ShapeDtypeStruct((states, rows, lanes), jnp.float32),
        ],
    )(inject_rows, read_rows, dt3, inj3, a3)
    return end3.reshape(states, channels), read3.reshape(steps, channels)


def ssm_correct(local_read, local_end, deltas, rates, read_rows):
    mine = lax.axis_index(SEQ)
    running = jnp.cumsum(deltas, axis=0)
    ends = lax.all_gather(local_end, SEQ)
    sums = lax.all_gather(running[-1], SEQ)
    devices = sums.shape[0]
    order = jnp.arange(devices, dtype=jnp.int32)
    masked = jnp.where((order < mine)[:, None], sums, 0.0)
    after = jnp.sum(masked, axis=0)[None, :] - jnp.cumsum(masked, axis=0)
    after = jnp.maximum(after, 0.0)
    carry = jnp.exp(rates[None] * after[:, None, :]) * ends
    incoming = jnp.sum(jnp.where((order < mine)[:, None, None], carry, 0.0), axis=0)
    growth = jnp.exp(rates[None] * running[:, None, :]) * incoming[None]
    fix = jnp.sum(read_rows.T[:, :, None] * growth, axis=1)
    return (local_read + fix).astype(jnp.bfloat16)


def attend(queries, window, query_pos, key_pos):
    count = queries.shape[0]
    key_count = window.shape[0]
    repeat = HQ // HK
    query_head_tensor = queries.reshape(count, HK, repeat, HEAD_SIZE)
    key_head_tensor = window[:, : HK * HEAD_SIZE].reshape(key_count, HK, HEAD_SIZE)
    value_head_tensor = window[:, HK * HEAD_SIZE :].reshape(key_count, HK, HEAD_SIZE)
    attention_scores = jnp.einsum(
        "bajq,oaq->ajbo", query_head_tensor, key_head_tensor, preferred_element_type=jnp.float32
    ) / math.sqrt(HEAD_SIZE)
    allowed = (key_pos[None, :] >= 0) & (key_pos[None, :] <= query_pos[:, None])
    attention_scores = jnp.where(allowed[None, None], attention_scores, -jnp.inf)
    row_max = jnp.max(attention_scores, axis=-1, keepdims=True)
    expd = jnp.exp(attention_scores - row_max)
    probabilities = (expd / jnp.sum(expd, axis=-1, keepdims=True)).astype(jnp.bfloat16)
    expert_mixture = jnp.einsum(
        "kyje,eku->jkyu", probabilities, value_head_tensor, preferred_element_type=jnp.float32
    )
    return expert_mixture.reshape(count, HQ * HEAD_SIZE).astype(jnp.bfloat16)


def expert_partial(gathered, w_gate, w_up, w_down):
    gate_pre = jnp.dot(gathered, w_gate, preferred_element_type=jnp.float32)
    up_pre = jnp.dot(gathered, w_up, preferred_element_type=jnp.float32)
    hidden_act = (jax.nn.silu(gate_pre) * up_pre).astype(jnp.bfloat16)
    return jnp.dot(hidden_act, w_down, preferred_element_type=jnp.float32).astype(jnp.bfloat16)


def body(
    ssm_in,
    ssm_dt,
    ssm_a,
    ssm_b,
    ssm_c,
    attn_q,
    attn_kv,
    moe_in,
    moe_routes,
    moe_prob,
    w_gate,
    w_up,
    w_down,
    *,
    seq_count,
):
    values = ssm_in.astype(jnp.float32)
    deltas = ssm_dt.astype(jnp.float32)
    local_end, local_read = sweep(values, deltas, ssm_a, ssm_b, ssm_c)
    ssm_out = ssm_correct(local_read, local_end, deltas, ssm_a, ssm_c)
    count = attn_q.shape[0]
    block_index = lax.axis_index(SEQ)
    one_back = shifted(attn_kv, SEQ, 1, seq_count)
    two_back = shifted(attn_kv, SEQ, 2, seq_count)
    window = jnp.concatenate([two_back, one_back, attn_kv], axis=0)
    first_row = block_index * count
    query_pos = first_row + jnp.arange(count, dtype=jnp.int32)
    key_pos = first_row - 2 * count + jnp.arange(3 * count, dtype=jnp.int32)
    attn_out = attend(attn_q, window, query_pos, key_pos)
    stream = (
        moe_in.astype(jnp.float32) + ssm_out.astype(jnp.float32) + attn_out.astype(jnp.float32)
    ).astype(jnp.bfloat16)
    local_tokens = stream.shape[0]
    width = stream.shape[1]
    group = seq_count // EXP_WIN
    expert_ids = jnp.arange(EXP_WIN, dtype=jnp.int32)
    matches = moe_routes[:, :, None] == expert_ids[None, None, :]
    routed = jnp.any(matches, axis=1).astype(jnp.int32)
    route_share = jnp.sum(jnp.where(matches, moe_prob[:, :, None], 0.0), axis=1)
    position_rank = jnp.cumsum(routed, axis=0) - 1
    picker = (routed[:, :, None] == 1) & (
        position_rank[:, :, None] == jnp.arange(SLOTS, dtype=jnp.int32)[None, None, :]
    )
    packed = jnp.einsum(
        "tek,td->ekd", picker.astype(jnp.bfloat16), stream, preferred_element_type=jnp.float32
    ).astype(jnp.bfloat16)
    by_expert = lax.all_to_all(packed, "eg", split_axis=0, concat_axis=0, tiled=True)
    outgoing = jnp.broadcast_to(by_expert[:, None], (EXP_WIN, group) + by_expert.shape[1:])
    arrived = lax.all_to_all(outgoing, "kg", split_axis=1, concat_axis=1, tiled=True)
    gathered = arrived.reshape(-1, width)
    partial_value = expert_partial(gathered, w_gate, w_up, w_down)
    returned = lax.all_to_all(
        partial_value.reshape((seq_count,) + arrived.shape[2:]), SEQ, split_axis=0, concat_axis=0, tiled=True
    )
    weighting = picker.astype(jnp.float32) * route_share[:, :, None]
    weighting = jnp.broadcast_to(
        weighting[:, :, None, :], (local_tokens, EXP_WIN, group, SLOTS)
    ).reshape(local_tokens, -1)
    combined = jnp.dot(
        weighting,
        returned.reshape(-1, width).astype(jnp.float32),
        precision=lax.Precision.HIGHEST,
        preferred_element_type=jnp.float32,
    )
    moe_out = combined.astype(jnp.bfloat16)
    return (ssm_out, attn_out, moe_out)


def solution(mesh):
    groups = mesh.shape["grp"]
    seq_count = mesh.shape["seq"]
    fine = Mesh(
        mesh.devices.reshape(groups, EXP_WIN, seq_count // EXP_WIN), ("grp",) + SEQ
    )
    rows = P(("grp",) + SEQ, None)
    return jax.shard_map(
        functools.partial(body, seq_count=seq_count),
        mesh=fine,
        in_specs=(
            rows,
            rows,
            P(),
            P(None, ("grp",) + SEQ),
            P(None, ("grp",) + SEQ),
            rows,
            rows,
            rows,
            rows,
            rows,
            P(None, SEQ),
            P(None, SEQ),
            P(SEQ, None),
        ),
        out_specs=(rows, rows, rows),
        check_vma=False,
    )
```

```python
import functools
import math

import jax
import jax.numpy as jnp
from jax import lax
from jax.experimental import pallas as pl
from jax.experimental.pallas import tpu as pltpu
from jax.sharding import Mesh, PartitionSpec as P

HQ = 32
HK = 8
HEAD_SIZE = 128
EXP_WIN = 4
CAP = 12
SLOTS = -(-CAP // 16) * 16
SEQ = ("eg", "kg")


def shifted(value, axis, by, devices):
    pairs = [(i, i + by) for i in range(devices) if 0 <= i + by < devices]
    return lax.ppermute(value, axis, pairs)


def scan_kernel(b_ref, c_ref, dt_ref, inj_ref, a_ref, read_ref, end_ref):
    states = a_ref.shape[0]
    steps = dt_ref.shape[0]
    h = [jnp.zeros(dt_ref.shape[1:], jnp.float32) for _ in range(states)]
    for t in range(steps):
        d = dt_ref[t].astype(jnp.float32)
        u = d * inj_ref[t].astype(jnp.float32)
        total = None
        for n in range(states):
            h[n] = jnp.exp(d * a_ref[n]) * h[n] + b_ref[n, t] * u
            term = c_ref[n, t] * h[n]
            total = term if total is None else total + term
        read_ref[t] = total
    for n in range(states):
        end_ref[n] = h[n]


def sweep(values, deltas, rates, inject_rows, read_rows):
    steps, channels = deltas.shape
    states = rates.shape[0]
    lanes = 128
    rows = channels // lanes
    tile = 16
    dt3 = deltas.reshape(steps, rows, lanes)
    inj3 = values.reshape(steps, rows, lanes)
    a3 = rates.reshape(states, rows, lanes)
    read3, end3 = pl.pallas_call(
        scan_kernel,
        grid=(rows // tile,),
        in_specs=[
            pl.BlockSpec(memory_space=pltpu.SMEM),
            pl.BlockSpec(memory_space=pltpu.SMEM),
            pl.BlockSpec((steps, tile, lanes), lambda j: (0, j, 0)),
            pl.BlockSpec((steps, tile, lanes), lambda j: (0, j, 0)),
            pl.BlockSpec((states, tile, lanes), lambda j: (0, j, 0)),
        ],
        out_specs=[
            pl.BlockSpec((steps, tile, lanes), lambda j: (0, j, 0)),
            pl.BlockSpec((states, tile, lanes), lambda j: (0, j, 0)),
        ],
        out_shape=[
            jax.ShapeDtypeStruct((steps, rows, lanes), jnp.float32),
            jax.ShapeDtypeStruct((states, rows, lanes), jnp.float32),
        ],
    )(inject_rows, read_rows, dt3, inj3, a3)
    return end3.reshape(states, channels), read3.reshape(steps, channels)


def ssm_correct(local_read, local_end, deltas, rates, read_rows):
    mine = lax.axis_index(SEQ)
    running = jnp.cumsum(deltas, axis=0)
    ends = lax.all_gather(local_end, SEQ)
    sums = lax.all_gather(running[-1], SEQ)
    devices = sums.shape[0]
    order = jnp.arange(devices, dtype=jnp.int32)
    masked = jnp.where((order < mine)[:, None], sums, 0.0)
    after = jnp.sum(masked, axis=0)[None, :] - jnp.cumsum(masked, axis=0)
    after = jnp.maximum(after, 0.0)
    carry = jnp.exp(rates[None] * after[:, None, :]) * ends
    incoming = jnp.sum(jnp.where((order < mine)[:, None, None], carry, 0.0), axis=0)
    growth = jnp.exp(rates[None] * running[:, None, :]) * incoming[None]
    fix = jnp.sum(read_rows.T[:, :, None] * growth, axis=1)
    return (local_read + fix).astype(jnp.bfloat16)


def attend(queries, window, query_pos, key_pos):
    count = queries.shape[0]
    key_count = window.shape[0]
    repeat = HQ // HK
    query_head_tensor = queries.reshape(count, HK, repeat, HEAD_SIZE)
    key_head_tensor = window[:, : HK * HEAD_SIZE].reshape(key_count, HK, HEAD_SIZE)
    value_head_tensor = window[:, HK * HEAD_SIZE :].reshape(key_count, HK, HEAD_SIZE)
    attention_scores = jnp.einsum(
        "bajq,oaq->ajbo", query_head_tensor, key_head_tensor, preferred_element_type=jnp.float32
    ) / math.sqrt(HEAD_SIZE)
    allowed = (key_pos[None, :] >= 0) & (key_pos[None, :] <= query_pos[:, None])
    attention_scores = jnp.where(allowed[None, None], attention_scores, -jnp.inf)
    row_max = jnp.max(attention_scores, axis=-1, keepdims=True)
    expd = jnp.exp(attention_scores - row_max)
    probabilities = (expd / jnp.sum(expd, axis=-1, keepdims=True)).astype(jnp.bfloat16)
    expert_mixture = jnp.einsum(
        "kyje,eku->jkyu", probabilities, value_head_tensor, preferred_element_type=jnp.float32
    )
    return expert_mixture.reshape(count, HQ * HEAD_SIZE).astype(jnp.bfloat16)


def expert_partial(gathered, w_gate, w_up, w_down):
    gate_pre = jnp.dot(gathered, w_gate, preferred_element_type=jnp.float32)
    up_pre = jnp.dot(gathered, w_up, preferred_element_type=jnp.float32)
    hidden_act = (jax.nn.silu(gate_pre) * up_pre).astype(jnp.bfloat16)
    return jnp.dot(hidden_act, w_down, preferred_element_type=jnp.float32).astype(jnp.bfloat16)


def body(
    ssm_in,
    ssm_dt,
    ssm_a,
    ssm_b,
    ssm_c,
    attn_q,
    attn_kv,
    moe_in,
    moe_routes,
    moe_prob,
    w_gate,
    w_up,
    w_down,
    *,
    seq_count,
):
    deltas = ssm_dt.astype(jnp.float32)
    local_end, local_read = sweep(ssm_in, ssm_dt, ssm_a, ssm_b, ssm_c)
    ssm_out = ssm_correct(local_read, local_end, deltas, ssm_a, ssm_c)
    count = attn_q.shape[0]
    block_index = lax.axis_index(SEQ)
    one_back = shifted(attn_kv, SEQ, 1, seq_count)
    two_back = shifted(attn_kv, SEQ, 2, seq_count)
    window = jnp.concatenate([two_back, one_back, attn_kv], axis=0)
    first_row = block_index * count
    query_pos = first_row + jnp.arange(count, dtype=jnp.int32)
    key_pos = first_row - 2 * count + jnp.arange(3 * count, dtype=jnp.int32)
    attn_out = attend(attn_q, window, query_pos, key_pos)
    stream = (
        moe_in.astype(jnp.float32) + ssm_out.astype(jnp.float32) + attn_out.astype(jnp.float32)
    ).astype(jnp.bfloat16)
    local_tokens = stream.shape[0]
    width = stream.shape[1]
    group = seq_count // EXP_WIN
    expert_ids = jnp.arange(EXP_WIN, dtype=jnp.int32)
    matches = moe_routes[:, :, None] == expert_ids[None, None, :]
    routed = jnp.any(matches, axis=1).astype(jnp.int32)
    route_share = jnp.sum(jnp.where(matches, moe_prob[:, :, None], 0.0), axis=1)
    position_rank = jnp.cumsum(routed, axis=0) - 1
    picker = (routed[:, :, None] == 1) & (
        position_rank[:, :, None] == jnp.arange(SLOTS, dtype=jnp.int32)[None, None, :]
    )
    packed = jnp.einsum(
        "tek,td->ekd", picker.astype(jnp.bfloat16), stream, preferred_element_type=jnp.float32
    ).astype(jnp.bfloat16)
    by_expert = lax.all_to_all(packed, "eg", split_axis=0, concat_axis=0, tiled=True)
    outgoing = jnp.broadcast_to(by_expert[:, None], (EXP_WIN, group) + by_expert.shape[1:])
    arrived = lax.all_to_all(outgoing, "kg", split_axis=1, concat_axis=1, tiled=True)
    gathered = arrived.reshape(-1, width)
    partial_value = expert_partial(gathered, w_gate, w_up, w_down)
    returned = lax.all_to_all(
        partial_value.reshape((seq_count,) + arrived.shape[2:]), SEQ, split_axis=0, concat_axis=0, tiled=True
    )
    summed = jnp.sum(returned.reshape(EXP_WIN, group, SLOTS, width), axis=1, dtype=jnp.float32)
    weighting = (picker.astype(jnp.float32) * route_share[:, :, None]).reshape(
        local_tokens, EXP_WIN * SLOTS
    )
    combined = jnp.dot(
        weighting,
        summed.reshape(EXP_WIN * SLOTS, width),
        precision=lax.Precision.HIGHEST,
        preferred_element_type=jnp.float32,
    )
    moe_out = combined.astype(jnp.bfloat16)
    return (ssm_out, attn_out, moe_out)


def solution(mesh):
    groups = mesh.shape["grp"]
    seq_count = mesh.shape["seq"]
    fine = Mesh(
        mesh.devices.reshape(groups, EXP_WIN, seq_count // EXP_WIN), ("grp",) + SEQ
    )
    rows = P(("grp",) + SEQ, None)
    return jax.shard_map(
        functools.partial(body, seq_count=seq_count),
        mesh=fine,
        in_specs=(
            rows,
            rows,
            P(),
            P(None, ("grp",) + SEQ),
            P(None, ("grp",) + SEQ),
            rows,
            rows,
            rows,
            rows,
            rows,
            P(None, SEQ),
            P(None, SEQ),
            P(SEQ, None),
        ),
        out_specs=(rows, rows, rows),
        check_vma=False,
    )
```

```python
import functools
import math

import jax
import jax.numpy as jnp
from jax import lax
from jax.experimental import pallas as pl
from jax.experimental.pallas import tpu as pltpu
from jax.sharding import Mesh, PartitionSpec as P

HQ = 32
HK = 8
HEAD_SIZE = 128
EXP_WIN = 4
CAP = 12
SLOTS = -(-CAP // 16) * 16
SEQ = ("eg", "kg")


def shifted(value, axis, by, devices):
    pairs = [(i, i + by) for i in range(devices) if 0 <= i + by < devices]
    return lax.ppermute(value, axis, pairs)


def scan_kernel(b_ref, c_ref, dt_ref, inj_ref, a_ref, read_ref, end_ref):
    states = a_ref.shape[0]
    steps = dt_ref.shape[0]
    h = [jnp.zeros(dt_ref.shape[1:], jnp.float32) for _ in range(states)]
    for t in range(steps):
        d = dt_ref[t]
        u = inj_ref[t]
        total = None
        for n in range(states):
            h[n] = jnp.exp(d * a_ref[n]) * h[n] + b_ref[n, t] * u
            term = c_ref[n, t] * h[n]
            total = term if total is None else total + term
        read_ref[t] = total
    for n in range(states):
        end_ref[n] = h[n]


def sweep(values, deltas, rates, inject_rows, read_rows):
    steps, channels = deltas.shape
    states = rates.shape[0]
    lanes = 128
    rows = channels // lanes
    tile = 16
    dt3 = deltas.reshape(steps, rows, lanes)
    inj3 = (deltas * values).reshape(steps, rows, lanes)
    a3 = rates.reshape(states, rows, lanes)
    read3, end3 = pl.pallas_call(
        scan_kernel,
        grid=(rows // tile,),
        in_specs=[
            pl.BlockSpec(memory_space=pltpu.SMEM),
            pl.BlockSpec(memory_space=pltpu.SMEM),
            pl.BlockSpec((steps, tile, lanes), lambda j: (0, j, 0)),
            pl.BlockSpec((steps, tile, lanes), lambda j: (0, j, 0)),
            pl.BlockSpec((states, tile, lanes), lambda j: (0, j, 0)),
        ],
        out_specs=[
            pl.BlockSpec((steps, tile, lanes), lambda j: (0, j, 0)),
            pl.BlockSpec((states, tile, lanes), lambda j: (0, j, 0)),
        ],
        out_shape=[
            jax.ShapeDtypeStruct((steps, rows, lanes), jnp.float32),
            jax.ShapeDtypeStruct((states, rows, lanes), jnp.float32),
        ],
    )(inject_rows, read_rows, dt3, inj3, a3)
    return end3.reshape(states, channels), read3.reshape(steps, channels)


def ssm_correct(local_read, local_end, deltas, rates, read_rows):
    mine = lax.axis_index(SEQ)
    running = jnp.cumsum(deltas, axis=0)
    ends = lax.all_gather(local_end, SEQ)
    sums = lax.all_gather(running[-1], SEQ)
    devices = sums.shape[0]
    order = jnp.arange(devices, dtype=jnp.int32)
    masked = jnp.where((order < mine)[:, None], sums, 0.0)
    after = jnp.sum(masked, axis=0)[None, :] - jnp.cumsum(masked, axis=0)
    after = jnp.maximum(after, 0.0)
    carry = jnp.exp(rates[None] * after[:, None, :]) * ends
    incoming = jnp.sum(jnp.where((order < mine)[:, None, None], carry, 0.0), axis=0)
    growth = jnp.exp(rates[None] * running[:, None, :]) * incoming[None]
    fix = jnp.sum(read_rows.T[:, :, None] * growth, axis=1)
    return (local_read + fix).astype(jnp.bfloat16)


def attend(queries, window, query_pos, key_pos):
    count = queries.shape[0]
    key_count = window.shape[0]
    repeat = HQ // HK
    query_head_tensor = queries.reshape(count, HK, repeat, HEAD_SIZE)
    key_head_tensor = window[:, : HK * HEAD_SIZE].reshape(key_count, HK, HEAD_SIZE)
    value_head_tensor = window[:, HK * HEAD_SIZE :].reshape(key_count, HK, HEAD_SIZE)
    attention_scores = jnp.einsum(
        "bajq,oaq->ajbo", query_head_tensor, key_head_tensor, preferred_element_type=jnp.float32
    ) / math.sqrt(HEAD_SIZE)
    allowed = (key_pos[None, :] >= 0) & (key_pos[None, :] <= query_pos[:, None])
    attention_scores = jnp.where(allowed[None, None], attention_scores, -jnp.inf)
    row_max = jnp.max(attention_scores, axis=-1, keepdims=True)
    expd = jnp.exp(attention_scores - row_max)
    probabilities = (expd / jnp.sum(expd, axis=-1, keepdims=True)).astype(jnp.bfloat16)
    expert_mixture = jnp.einsum(
        "kyje,eku->jkyu", probabilities, value_head_tensor, preferred_element_type=jnp.float32
    )
    return expert_mixture.reshape(count, HQ * HEAD_SIZE).astype(jnp.bfloat16)


def expert_partial(gathered, w_gate, w_up, w_down):
    gate_pre = jnp.dot(gathered, w_gate, preferred_element_type=jnp.float32)
    up_pre = jnp.dot(gathered, w_up, preferred_element_type=jnp.float32)
    hidden_act = (jax.nn.silu(gate_pre) * up_pre).astype(jnp.bfloat16)
    return jnp.dot(hidden_act, w_down, preferred_element_type=jnp.float32).astype(jnp.bfloat16)


def body(
    ssm_in,
    ssm_dt,
    ssm_a,
    ssm_b,
    ssm_c,
    attn_q,
    attn_kv,
    moe_in,
    moe_routes,
    moe_prob,
    w_gate,
    w_up,
    w_down,
    *,
    seq_count,
):
    values = ssm_in.astype(jnp.float32)
    deltas = ssm_dt.astype(jnp.float32)
    local_end, local_read = sweep(values, deltas, ssm_a, ssm_b, ssm_c)
    ssm_out = ssm_correct(local_read, local_end, deltas, ssm_a, ssm_c)
    count = attn_q.shape[0]
    block_index = lax.axis_index(SEQ)
    one_back = shifted(attn_kv, SEQ, 1, seq_count)
    two_back = shifted(attn_kv, SEQ, 2, seq_count)
    window = jnp.concatenate([two_back, one_back, attn_kv], axis=0)
    first_row = block_index * count
    query_pos = first_row + jnp.arange(count, dtype=jnp.int32)
    key_pos = first_row - 2 * count + jnp.arange(3 * count, dtype=jnp.int32)
    attn_out = attend(attn_q, window, query_pos, key_pos)
    stream = (
        moe_in.astype(jnp.float32) + ssm_out.astype(jnp.float32) + attn_out.astype(jnp.float32)
    ).astype(jnp.bfloat16)
    local_tokens = stream.shape[0]
    width = stream.shape[1]
    group = seq_count // EXP_WIN
    expert_ids = jnp.arange(EXP_WIN, dtype=jnp.int32)
    matches = moe_routes[:, :, None] == expert_ids[None, None, :]
    routed = jnp.any(matches, axis=1).astype(jnp.int32)
    route_share = jnp.sum(jnp.where(matches, moe_prob[:, :, None], 0.0), axis=1)
    position_rank = jnp.cumsum(routed, axis=0) - 1
    picker = (routed[:, :, None] == 1) & (
        position_rank[:, :, None] == jnp.arange(SLOTS, dtype=jnp.int32)[None, None, :]
    )
    packed = jnp.einsum(
        "tek,td->ekd", picker.astype(jnp.bfloat16), stream, preferred_element_type=jnp.float32
    ).astype(jnp.bfloat16)
    by_expert = lax.all_to_all(packed, "eg", split_axis=0, concat_axis=0, tiled=True)
    outgoing = jnp.broadcast_to(by_expert[:, None], (EXP_WIN, group) + by_expert.shape[1:])
    arrived = lax.all_to_all(outgoing, "kg", split_axis=1, concat_axis=1, tiled=True)
    gathered = arrived.reshape(-1, width)
    partial_value = expert_partial(gathered, w_gate, w_up, w_down)
    returned = lax.all_to_all(
        partial_value.reshape((seq_count,) + arrived.shape[2:]), SEQ, split_axis=0, concat_axis=0, tiled=True
    )
    summed = jnp.sum(returned.reshape(EXP_WIN, group, SLOTS, width), axis=1, dtype=jnp.float32)
    weighting = (picker.astype(jnp.float32) * route_share[:, :, None]).reshape(
        local_tokens, EXP_WIN * SLOTS
    )
    combined = jnp.dot(
        weighting,
        summed.reshape(EXP_WIN * SLOTS, width),
        precision=lax.Precision.HIGHEST,
        preferred_element_type=jnp.float32,
    )
    moe_out = combined.astype(jnp.bfloat16)
    return (ssm_out, attn_out, moe_out)


def solution(mesh):
    groups = mesh.shape["grp"]
    seq_count = mesh.shape["seq"]
    fine = Mesh(
        mesh.devices.reshape(groups, EXP_WIN, seq_count // EXP_WIN), ("grp",) + SEQ
    )
    rows = P(("grp",) + SEQ, None)
    return jax.shard_map(
        functools.partial(body, seq_count=seq_count),
        mesh=fine,
        in_specs=(
            rows,
            rows,
            P(),
            P(None, ("grp",) + SEQ),
            P(None, ("grp",) + SEQ),
            rows,
            rows,
            rows,
            rows,
            rows,
            P(None, SEQ),
            P(None, SEQ),
            P(SEQ, None),
        ),
        out_specs=(rows, rows, rows),
        check_vma=False,
    )
```
